512 devices in a mesh: bulk: 32 (over z, core), seg: 16 (over y, x).
Axes of the slice: x: 4, y: 4, z: 16, core: 2. Of those that a mesh axis runs over, the one named last changes fastest.
Arguments:
- em_cutouts: bfloat16 [32, 16, 40, 4096], P('bulk', 'seg'), may hold values from -6 to 6
- mask_cutouts: bfloat16 [32, 16, 40, 2, 4096], P('bulk', 'seg'), may hold values from 0 to 1
- live_count: int32 [32, 16], replicated, may hold values from 1 to 40, as said below
- segment_ids: int32 [32, 16, 40], P('bulk', 'seg'), may hold values from 0 to 127
- patch_weight: bfloat16 [32, 24], replicated, may hold values from -1.75 to 1.75
- conv_weight: bfloat16 [3, 27, 32, 32], replicated, may hold values from -0.3125 to 0.3125
- conv_bias: float32 [4, 32], replicated, may hold values from -3 to 3
- score_weight: float32 [32], replicated, may hold values from -2 to 2
- embed_weight: bfloat16 [32, 128], replicated, may hold values from -1 to 1
Outputs:
- pair_score: bfloat16 [32, 16, 40], P('bulk', 'seg')
- segment_embed: float32 [4096, 128], P(('bulk', 'seg'))
The draws below stay inside these ranges and needn't reach their ends.
Inputs may be any that keep to these rules, and one draw needn't show every extreme that they name: `live_count`: along bulk, the 32 devices of each seg column hold 320 live slots in all, and one device of every column holds 40; so every owner scores exactly 10 pairs and gets at most 2 from any one device.
All inputs are finite; a program needn't handle non-finite values.
Results may differ from the reference program's by a relative error of at most 0.012.
Values may be sent and summed in bfloat16 or wider, within the bound.
No kernel may reach another device: no remote copies, remote signals or barrier semaphores. Data moves between devices by JAX's collectives and lax.ppermute only.
A program may use at most 192 MiB of HBM per device.

```python
import jax
import jax.numpy as jnp
from jax import lax

PAIR_DEV = 10
CUT_DEV = 40
CS = 16
VOX_CUT = 4096
CH = 32
EMB = 128
LAYERS = 3
SEGS_ROW = 128
SEGS = 4096
N_BULK = 32
N_SEG = 16


def draw_live_count(key, part):
    key_top = jax.random.fold_in(key, 11)
    key_weight = jax.random.fold_in(key, 12)
    top_row = jax.random.randint(key_top, (1, N_SEG), 0, N_BULK)
    row_ids = jnp.arange(N_BULK, dtype=jnp.int32)[:, None]
    is_top = row_ids == top_row
    weights = jax.random.randint(key_weight, (N_BULK, N_SEG), 4, 8)
    weights = jnp.where(is_top, 0, weights)
    leftover = N_BULK * PAIR_DEV - CUT_DEV - (N_BULK - 1)
    base = leftover * weights // jnp.sum(weights, axis=0, keepdims=True)
    remain = leftover - jnp.sum(base, axis=0, keepdims=True)
    others = jnp.where(is_top, 0, 1)
    order = jnp.cumsum(others, axis=0) - 1
    extra = jnp.where((order < remain) & (others == 1), 1, 0)
    counts = jnp.where(is_top, CUT_DEV, 1 + base + extra)
    return counts.astype(jnp.int32)


def place_ends(drawn, own_key, least, top_value):
    spot = [jax.random.randint(jax.random.fold_in(own_key, axis), (), 0, length) for axis, length in enumerate(drawn.shape)]
    main_axis = drawn.shape.index(max(drawn.shape))
    neighbour = spot[:main_axis] + [(spot[main_axis] + 1) % drawn.shape[main_axis]] + spot[main_axis + 1:]
    return drawn.at[tuple(spot)].set(least).at[tuple(neighbour)].set(top_value)


def shard_levels(key, shape, shards, least, largest):
    level = 1.0
    for dim, parts in shards:
        heights = jax.random.uniform(jax.random.fold_in(jax.random.fold_in(key, 6), dim), (parts,), jnp.float32, least / len(shards), largest / len(shards))
        level = level * jnp.repeat(jnp.exp(heights), shape[dim] // parts).reshape((-1,) + (1,) * (len(shape) - 1 - dim))
    return level


def centred(stream_key, shape, spread, most, pieces=(), kind=jnp.bfloat16):
    values = spread * jax.random.normal(stream_key, shape, jnp.float32)
    if pieces:
        values = values * shard_levels(stream_key, shape, pieces, -0.22, 0.18)
    return jnp.clip(values, -most, most).astype(kind)


def setup_inputs(seed: int = 0) -> dict:
    key_of = jax.random.split(jax.random.key(seed), 10)
    return {
        "em_cutouts": centred(key_of[0], (N_BULK, N_SEG, CUT_DEV, VOX_CUT), 1.0, 6.0, ((0, 32), (1, 16))),
        "mask_cutouts": jnp.clip(1.0 * jax.random.uniform(key_of[1], (N_BULK, N_SEG, CUT_DEV, 2, VOX_CUT), jnp.float32) ** shard_levels(key_of[1], (N_BULK, N_SEG, CUT_DEV, 2, VOX_CUT), ((0, 32), (1, 16)), -0.2, 0.2), 0.0, 1.0).astype(jnp.bfloat16),
        "live_count": draw_live_count(jax.random.fold_in(key_of[9], 71), 0),
        "segment_ids": place_ends(jax.random.randint(key_of[3], (N_BULK, N_SEG, CUT_DEV), 0, SEGS_ROW), jax.random.fold_in(key_of[3], 1), 0, SEGS_ROW - 1).astype(jnp.int32),
        "patch_weight": centred(key_of[4], (CH, 24), 12 ** -0.5, 1.75),
        "conv_weight": centred(key_of[5], (LAYERS, 27, CH, CH), (27 * CH // 2) ** -0.5, 0.3125),
        "conv_bias": centred(key_of[6], (LAYERS + 1, CH), 0.5, 3.0, (), jnp.float32),
        "score_weight": centred(key_of[7], (CH,), (CH // 4) ** -0.5, 2.0, (), jnp.float32),
        "embed_weight": centred(key_of[8], (CH, EMB), CH ** -0.5, 1.0),
    }


def run_network(em_rows, mask_rows, patch_weight, conv_weight, conv_bias, score_weight, embed_weight):
    rows_here = em_rows.shape[0]
    side_half = CS // 2
    voxel_count = side_half * side_half * side_half
    channels = conv_weight.shape[2]
    highest = lax.Precision.HIGHEST
    stacked = jnp.concatenate([em_rows[:, None, :], mask_rows], axis=1)
    blocks = stacked.reshape(rows_here, 3, side_half, 2, side_half, 2, side_half, 2)
    blocks = blocks.transpose(0, 1, 3, 5, 7, 2, 4, 6).reshape(rows_here, 24, voxel_count)
    first_out = jnp.einsum("of,pfv->pov", patch_weight.astype(jnp.float32), blocks.astype(jnp.float32), precision=highest)
    hidden = jax.nn.relu(first_out + conv_bias[0][None, :, None]).astype(jnp.bfloat16)
    for layer_index in range(LAYERS):
        volume = hidden.reshape(rows_here, channels, side_half, side_half, side_half)
        padded = jnp.pad(volume, ((0, 0), (0, 0), (1, 1), (1, 1), (1, 1)))
        summed_taps = jnp.zeros((rows_here, channels, voxel_count), jnp.float32)
        for tap_index in range(27):
            shift_x = tap_index // 9
            shift_y = (tap_index // 3) % 3
            shift_z = tap_index % 3
            window = padded[:, :, shift_x:shift_x + side_half, shift_y:shift_y + side_half, shift_z:shift_z + side_half]
            window = window.reshape(rows_here, channels, voxel_count)
            summed_taps = summed_taps + jnp.einsum("oc,pcv->pov", conv_weight[layer_index, tap_index].astype(jnp.float32), window.astype(jnp.float32), precision=highest)
        hidden = jax.nn.relu(summed_taps + conv_bias[layer_index + 1][None, :, None]).astype(jnp.bfloat16)
    intersection = mask_rows[:, 0].astype(jnp.float32) * mask_rows[:, 1].astype(jnp.float32)
    intersection = intersection.reshape(rows_here, side_half, 2, side_half, 2, side_half, 2)
    boundary = jnp.mean(intersection, axis=(2, 4, 6)).reshape(rows_here, voxel_count) + 0.1
    pooled = jnp.einsum("pcv,pv->pc", hidden.astype(jnp.float32), boundary, precision=highest)
    pooled = pooled / jnp.sum(boundary, axis=1, keepdims=True)
    logits = jnp.dot(pooled, score_weight, precision=highest)
    scores = jax.nn.sigmoid(logits).astype(jnp.bfloat16)
    embedded = jnp.tanh(jnp.dot(pooled, embed_weight.astype(jnp.float32), precision=highest))
    contrib = (scores.astype(jnp.float32)[:, None] * embedded).astype(jnp.bfloat16)
    return scores, contrib


def reference(em_cutouts, mask_cutouts, live_count, segment_ids, patch_weight, conv_weight, conv_bias, score_weight, embed_weight):
    slot_ids = jnp.arange(CUT_DEV, dtype=jnp.int32)
    live_slot = slot_ids[None, None, :] < live_count[:, :, None]
    flat_alive = live_slot.reshape(-1)
    total_pairs = N_BULK * N_SEG * PAIR_DEV
    all_slots = N_BULK * N_SEG * CUT_DEV
    picked_ids = jnp.nonzero(flat_alive, size=total_pairs)[0].astype(jnp.int32)
    em_flat = em_cutouts.reshape(all_slots, VOX_CUT)
    mask_flat = mask_cutouts.reshape(all_slots, 2, VOX_CUT)

    def score_block(block_ids):
        return run_network(em_flat[block_ids], mask_flat[block_ids], patch_weight, conv_weight, conv_bias, score_weight, embed_weight)

    scores, contribs = lax.map(score_block, picked_ids.reshape(-1, 32))
    scores = scores.reshape(total_pairs)
    contribs = contribs.reshape(total_pairs, EMB)
    pair_score = jnp.zeros((all_slots,), jnp.bfloat16).at[picked_ids].set(scores)
    pair_score = pair_score.reshape(N_BULK, N_SEG, CUT_DEV)
    row_of = jnp.arange(all_slots, dtype=jnp.int32) // (N_SEG * CUT_DEV)
    seg_global = row_of * SEGS_ROW + segment_ids.reshape(-1).astype(jnp.int32)
    segment_embed = jax.ops.segment_sum(contribs.astype(jnp.float32), seg_global[picked_ids], num_segments=SEGS)
    return pair_score, segment_embed
```

```python
import jax
import jax.numpy as jnp
from jax import lax
from jax.sharding import PartitionSpec as P

CS = 16
LAYERS = 3
SEG_DEV = 8


def run_network(
    em_rows, mask_rows, patch_weight, conv_weight, conv_bias, score_weight, embed_weight
):
    rows_here = em_rows.shape[0]
    side_half = CS // 2
    voxel_count = side_half * side_half * side_half
    channels = conv_weight.shape[2]
    highest = lax.Precision.HIGHEST
    stacked = jnp.concatenate([em_rows[:, None, :], mask_rows], axis=1)
    volume_in = stacked.reshape(rows_here, 3, CS, CS, CS)
    patch_kernel = patch_weight.reshape(channels, 3, 2, 2, 2)
    first_out = lax.conv_general_dilated(
        volume_in,
        patch_kernel,
        (2, 2, 2),
        "VALID",
        dimension_numbers=("NCDHW", "OIDHW", "NDHWC"),
        preferred_element_type=jnp.float32,
    )
    volume = jax.nn.relu(first_out + conv_bias[0]).astype(jnp.bfloat16)
    for layer_index in range(LAYERS):
        kernel = conv_weight[layer_index].reshape(3, 3, 3, channels, channels).transpose(0, 1, 2, 4, 3)
        summed_taps = lax.conv_general_dilated(
            volume,
            kernel,
            (1, 1, 1),
            ((1, 1), (1, 1), (1, 1)),
            dimension_numbers=("NDHWC", "DHWIO", "NDHWC"),
            preferred_element_type=jnp.float32,
        )
        volume = jax.nn.relu(summed_taps + conv_bias[layer_index + 1]).astype(jnp.bfloat16)
    hidden = volume.reshape(rows_here, voxel_count, channels)
    intersection = mask_rows[:, 0].astype(jnp.float32) * mask_rows[:, 1].astype(jnp.float32)
    intersection = intersection.reshape(rows_here, side_half, 2, side_half, 2, side_half, 2)
    boundary = jnp.mean(intersection, axis=(2, 4, 6)).reshape(rows_here, voxel_count) + 0.1
    pooled = jnp.einsum("pvc,pv->pc", hidden.astype(jnp.float32), boundary, precision=highest)
    pooled = pooled / jnp.sum(boundary, axis=1, keepdims=True)
    logits = jnp.dot(pooled, score_weight, precision=highest)
    scores = jax.nn.sigmoid(logits).astype(jnp.bfloat16)
    embedded = jnp.tanh(jnp.dot(pooled, embed_weight.astype(jnp.float32), precision=highest))
    contrib = (scores.astype(jnp.float32)[:, None] * embedded).astype(jnp.bfloat16)
    return (scores, contrib)


def per_device(
    em_cutouts,
    mask_cutouts,
    live_count,
    segment_ids,
    patch_weight,
    conv_weight,
    conv_bias,
    score_weight,
    embed_weight,
):
    bulk_index = lax.axis_index("bulk")
    seg_index = lax.axis_index("seg")
    slots = em_cutouts.shape[2]
    em_local = em_cutouts.reshape(slots, -1)
    mask_local = mask_cutouts.reshape(slots, 2, -1)
    own_count = live_count[bulk_index, seg_index]
    slot_ids = jnp.arange(slots, dtype=jnp.int32)
    live_slot = slot_ids < own_count
    part_score, part_contrib = run_network(
        em_local, mask_local, patch_weight, conv_weight, conv_bias, score_weight, embed_weight
    )
    scores = jnp.where(live_slot, part_score, 0)
    contribs = jnp.where(live_slot[:, None], part_contrib, 0)
    seg_local = jnp.where(live_slot, segment_ids.reshape(slots), -1)
    packed = jnp.concatenate([contribs, seg_local[:, None].astype(jnp.bfloat16)], axis=1)
    gathered = lax.all_gather(packed, "seg", tiled=True)
    all_contrib = gathered[:, :-1]
    all_ids = gathered[:, -1].astype(jnp.int32)
    wanted = seg_index * SEG_DEV + jnp.arange(SEG_DEV, dtype=jnp.int32)
    onehot = (all_ids[None, :] == wanted[:, None]).astype(jnp.bfloat16)
    summed = jnp.dot(onehot, all_contrib, preferred_element_type=jnp.float32)
    return (scores.reshape(1, 1, slots), summed)


def solution(mesh):
    in_specs = (
        P("bulk", "seg", None, None),
        P("bulk", "seg", None, None, None),
        P(),
        P("bulk", "seg", None),
        P(),
        P(),
        P(),
        P(),
        P(),
    )
    out_specs = (P("bulk", "seg", None), P(("bulk", "seg"), None))
    return jax.shard_map(
        per_device, mesh=mesh, in_specs=in_specs, out_specs=out_specs, check_vma=False
    )
```

```python
import jax
import jax.numpy as jnp
from jax import lax
from jax.sharding import PartitionSpec as P

CS = 16
LAYERS = 3
SEG_DEV = 8


def run_network(
    em_rows, mask_rows, patch_weight, conv_weight, conv_bias, score_weight, embed_weight
):
    rows_here = em_rows.shape[0]
    side_half = CS // 2
    voxel_count = side_half * side_half * side_half
    channels = conv_weight.shape[2]
    highest = lax.Precision.HIGHEST
    stacked = jnp.concatenate([em_rows[:, None, :], mask_rows], axis=1)
    volume_in = stacked.reshape(rows_here, 3, CS, CS, CS)
    patch_kernel = patch_weight.reshape(channels, 3, 2, 2, 2)
    first_out = lax.conv_general_dilated(
        volume_in,
        patch_kernel,
        (2, 2, 2),
        "VALID",
        dimension_numbers=("NCDHW", "OIDHW", "NDHWC"),
        preferred_element_type=jnp.float32,
    )
    lanes = side_half * channels
    volume = jax.nn.relu(first_out + conv_bias[0]).astype(jnp.bfloat16)
    volume = volume.reshape(rows_here, side_half, side_half, lanes)
    taps = conv_weight.reshape(LAYERS, 3, 3, 3, channels, channels)
    z_in = jnp.arange(side_half)[None, :, None]
    z_out = jnp.arange(side_half)[None, None, :]
    shift_c = jnp.arange(3)[:, None, None]
    band = (z_in - z_out + 1 == shift_c).astype(jnp.bfloat16)
    banded = jnp.einsum(
        "cuz,labcoi->labuizo", band, taps, preferred_element_type=jnp.float32
    ).astype(jnp.bfloat16)
    banded = banded.reshape(LAYERS, 3, 3, lanes, lanes)
    for layer_index in range(LAYERS):
        summed_taps = lax.conv_general_dilated(
            volume,
            banded[layer_index],
            (1, 1),
            ((1, 1), (1, 1)),
            dimension_numbers=("NHWC", "HWIO", "NHWC"),
            preferred_element_type=jnp.float32,
        )
        bias = jnp.tile(conv_bias[layer_index + 1], side_half)
        volume = jax.nn.relu(summed_taps + bias).astype(jnp.bfloat16)
    hidden = volume.reshape(rows_here, voxel_count, channels)
    intersection = mask_rows[:, 0].astype(jnp.float32) * mask_rows[:, 1].astype(jnp.float32)
    intersection = intersection.reshape(rows_here, side_half, 2, side_half, 2, side_half, 2)
    boundary = jnp.mean(intersection, axis=(2, 4, 6)).reshape(rows_here, voxel_count) + 0.1
    pooled = jnp.einsum("pvc,pv->pc", hidden.astype(jnp.float32), boundary, precision=highest)
    pooled = pooled / jnp.sum(boundary, axis=1, keepdims=True)
    logits = jnp.dot(pooled, score_weight, precision=highest)
    scores = jax.nn.sigmoid(logits).astype(jnp.bfloat16)
    embedded = jnp.tanh(jnp.dot(pooled, embed_weight.astype(jnp.float32), precision=highest))
    contrib = (scores.astype(jnp.float32)[:, None] * embedded).astype(jnp.bfloat16)
    return (scores, contrib)


def per_device(
    em_cutouts,
    mask_cutouts,
    live_count,
    segment_ids,
    patch_weight,
    conv_weight,
    conv_bias,
    score_weight,
    embed_weight,
):
    bulk_index = lax.axis_index("bulk")
    seg_index = lax.axis_index("seg")
    slots = em_cutouts.shape[2]
    em_local = em_cutouts.reshape(slots, -1)
    mask_local = mask_cutouts.reshape(slots, 2, -1)
    own_count = live_count[bulk_index, seg_index]
    slot_ids = jnp.arange(slots, dtype=jnp.int32)
    live_slot = slot_ids < own_count
    part_score, part_contrib = run_network(
        em_local, mask_local, patch_weight, conv_weight, conv_bias, score_weight, embed_weight
    )
    scores = jnp.where(live_slot, part_score, 0)
    contribs = jnp.where(live_slot[:, None], part_contrib, 0)
    seg_local = jnp.where(live_slot, segment_ids.reshape(slots), -1)
    packed = jnp.concatenate([contribs, seg_local[:, None].astype(jnp.bfloat16)], axis=1)
    gathered = lax.all_gather(packed, "seg", tiled=True)
    all_contrib = gathered[:, :-1]
    all_ids = gathered[:, -1].astype(jnp.int32)
    wanted = seg_index * SEG_DEV + jnp.arange(SEG_DEV, dtype=jnp.int32)
    onehot = (all_ids[None, :] == wanted[:, None]).astype(jnp.bfloat16)
    summed = jnp.dot(onehot, all_contrib, preferred_element_type=jnp.float32)
    return (scores.reshape(1, 1, slots), summed)


def solution(mesh):
    in_specs = (
        P("bulk", "seg", None, None),
        P("bulk", "seg", None, None, None),
        P(),
        P("bulk", "seg", None),
        P(),
        P(),
        P(),
        P(),
        P(),
    )
    out_specs = (P("bulk", "seg", None), P(("bulk", "seg"), None))
    return jax.shard_map(
        per_device, mesh=mesh, in_specs=in_specs, out_specs=out_specs, check_vma=False
    )
```

```python
import jax
import jax.numpy as jnp
from jax import lax
from jax.sharding import PartitionSpec as P

CS = 16
LAYERS = 3
SEG_DEV = 8


def run_network(
    em_rows, mask_rows, patch_weight, conv_weight, conv_bias, score_weight, embed_weight
):
    rows_here = em_rows.shape[0]
    side_half = CS // 2
    voxel_count = side_half * side_half * side_half
    channels = conv_weight.shape[2]
    highest = lax.Precision.HIGHEST
    stacked = jnp.concatenate([em_rows[:, None, :], mask_rows], axis=1)
    volume_in = stacked.reshape(rows_here, 3, CS, CS, CS)
    patch_kernel = patch_weight.reshape(channels, 3, 2, 2, 2)
    first_out = lax.conv_general_dilated(
        volume_in,
        patch_kernel,
        (2, 2, 2),
        "VALID",
        dimension_numbers=("NCDHW", "OIDHW", "NDHWC"),
        preferred_element_type=jnp.float32,
    )
    lanes = side_half * channels
    volume = jax.nn.relu(first_out + conv_bias[0]).astype(jnp.bfloat16)
    volume = volume.reshape(rows_here, side_half, side_half, lanes)
    taps = conv_weight.reshape(LAYERS, 3, 3, 3, channels, channels).transpose(0, 1, 2, 3, 5, 4)
    z_in = jnp.arange(side_half)[:, None, None, None]
    z_out = jnp.arange(side_half)[None, None, :, None]
    banded = []
    for layer_index in range(LAYERS):
        band = jnp.zeros((3, 3, side_half, channels, side_half, channels), jnp.bfloat16)
        for shift_c in range(3):
            hit = z_in - z_out + 1 == shift_c
            tap = taps[layer_index, :, :, shift_c][:, :, None, :, None, :]
            band = band + jnp.where(hit, tap, 0)
        banded.append(band.reshape(3, 3, lanes, lanes))
    for layer_index in range(LAYERS):
        summed_taps = lax.conv_general_dilated(
            volume,
            banded[layer_index],
            (1, 1),
            ((1, 1), (1, 1)),
            dimension_numbers=("NHWC", "HWIO", "NHWC"),
            preferred_element_type=jnp.float32,
        )
        bias = jnp.tile(conv_bias[layer_index + 1], side_half)
        volume = jax.nn.relu(summed_taps + bias).astype(jnp.bfloat16)
    hidden = volume.reshape(rows_here, voxel_count, channels)
    intersection = mask_rows[:, 0].astype(jnp.float32) * mask_rows[:, 1].astype(jnp.float32)
    intersection = intersection.reshape(rows_here, side_half, 2, side_half, 2, side_half, 2)
    boundary = jnp.mean(intersection, axis=(2, 4, 6)).reshape(rows_here, voxel_count) + 0.1
    pooled = jnp.einsum("pvc,pv->pc", hidden.astype(jnp.float32), boundary, precision=highest)
    pooled = pooled / jnp.sum(boundary, axis=1, keepdims=True)
    logits = jnp.dot(pooled, score_weight, precision=highest)
    scores = jax.nn.sigmoid(logits).astype(jnp.bfloat16)
    embedded = jnp.tanh(jnp.dot(pooled, embed_weight.astype(jnp.float32), precision=highest))
    contrib = (scores.astype(jnp.float32)[:, None] * embedded).astype(jnp.bfloat16)
    return (scores, contrib)


def per_device(
    em_cutouts,
    mask_cutouts,
    live_count,
    segment_ids,
    patch_weight,
    conv_weight,
    conv_bias,
    score_weight,
    embed_weight,
):
    bulk_index = lax.axis_index("bulk")
    seg_index = lax.axis_index("seg")
    slots = em_cutouts.shape[2]
    em_local = em_cutouts.reshape(slots, -1)
    mask_local = mask_cutouts.reshape(slots, 2, -1)
    own_count = live_count[bulk_index, seg_index]
    slot_ids = jnp.arange(slots, dtype=jnp.int32)
    live_slot = slot_ids < own_count
    part_score, part_contrib = run_network(
        em_local, mask_local, patch_weight, conv_weight, conv_bias, score_weight, embed_weight
    )
    scores = jnp.where(live_slot, part_score, 0)
    contribs = jnp.where(live_slot[:, None], part_contrib, 0)
    seg_local = jnp.where(live_slot, segment_ids.reshape(slots), -1)
    packed = jnp.concatenate([contribs, seg_local[:, None].astype(jnp.bfloat16)], axis=1)
    gathered = lax.all_gather(packed, "seg", tiled=True)
    all_contrib = gathered[:, :-1]
    all_ids = gathered[:, -1].astype(jnp.int32)
    wanted = seg_index * SEG_DEV + jnp.arange(SEG_DEV, dtype=jnp.int32)
    onehot = (all_ids[None, :] == wanted[:, None]).astype(jnp.bfloat16)
    summed = jnp.dot(onehot, all_contrib, preferred_element_type=jnp.float32)
    return (scores.reshape(1, 1, slots), summed)


def solution(mesh):
    in_specs = (
        P("bulk", "seg", None, None),
        P("bulk", "seg", None, None, None),
        P(),
        P("bulk", "seg", None),
        P(),
        P(),
        P(),
        P(),
        P(),
    )
    out_specs = (P("bulk", "seg", None), P(("bulk", "seg"), None))
    return jax.shard_map(
        per_device, mesh=mesh, in_specs=in_specs, out_specs=out_specs, check_vma=False
    )
```

```python
import jax
import jax.numpy as jnp
from jax import lax
from jax.sharding import PartitionSpec as P
from jax.experimental import pallas as pl
from jax.experimental.pallas import tpu as pltpu

CS = 16
LAYERS = 3
SEG_DEV = 8
BLOCK_PAIRS = 8
PAD_ROWS = 16


def conv_kernel(h_ref, w_ref, b_ref, o_ref, pad_ref, col_ref):
    rows, lanes = h_ref.shape
    side = CS // 2
    edge = PAD_ROWS
    pad_ref[0:edge, :] = jnp.zeros((edge, lanes), jnp.float32)
    pad_ref[edge + rows:, :] = jnp.zeros((edge, lanes), jnp.float32)
    pad_ref[edge:edge + rows, :] = h_ref[...].astype(jnp.float32)
    row_id = lax.broadcasted_iota(jnp.int32, (rows, lanes), 0)
    y_pos = row_id % side
    x_pos = (row_id // side) % side
    for layer_index in range(LAYERS):
        for shift_a in range(3):
            for shift_b in range(3):
                tap = shift_a * 3 + shift_b
                offset = (shift_a - 1) * side + (shift_b - 1)
                window = pad_ref[edge + offset:edge + offset + rows, :]
                x_to = x_pos + (shift_a - 1)
                y_to = y_pos + (shift_b - 1)
                inside = (x_to >= 0) & (x_to < side) & (y_to >= 0) & (y_to < side)
                col_ref[:, tap * lanes:(tap + 1) * lanes] = jnp.where(
                    inside, window, 0.0
                ).astype(jnp.bfloat16)
        summed = jnp.dot(col_ref[...], w_ref[layer_index], preferred_element_type=jnp.float32)
        hidden = jnp.maximum(summed + b_ref[layer_index], 0.0).astype(jnp.bfloat16)
        if layer_index + 1 < LAYERS:
            pad_ref[edge:edge + rows, :] = hidden.astype(jnp.float32)
        else:
            o_ref[...] = hidden


def conv_layers(volume, conv_weight, conv_bias):
    total_rows, lanes = volume.shape
    side = CS // 2
    channels = conv_weight.shape[2]
    taps = conv_weight.reshape(LAYERS, 3, 3, 3, channels, channels).transpose(0, 1, 2, 3, 5, 4)
    z_in = jnp.arange(side)[:, None, None, None]
    z_out = jnp.arange(side)[None, None, :, None]
    band = jnp.zeros((LAYERS, 3, 3, side, channels, side, channels), jnp.bfloat16)
    for shift_c in range(3):
        hit = z_in - z_out + 1 == shift_c
        band = band + jnp.where(hit, taps[:, :, :, shift_c][:, :, :, None, :, None, :], 0)
    band = band.reshape(LAYERS, 9 * lanes, lanes)
    bias = jnp.tile(conv_bias[1:], (1, side)).reshape(LAYERS, 1, lanes)
    block_rows = BLOCK_PAIRS * side * side
    return pl.pallas_call(
        conv_kernel,
        grid=(total_rows // block_rows,),
        in_specs=[
            pl.BlockSpec((block_rows, lanes), lambda i: (i, 0)),
            pl.BlockSpec((LAYERS, 9 * lanes, lanes), lambda i: (0, 0, 0)),
            pl.BlockSpec((LAYERS, 1, lanes), lambda i: (0, 0, 0)),
        ],
        out_specs=pl.BlockSpec((block_rows, lanes), lambda i: (i, 0)),
        out_shape=jax.ShapeDtypeStruct((total_rows, lanes), jnp.bfloat16),
        scratch_shapes=[
            pltpu.VMEM((block_rows + 2 * PAD_ROWS, lanes), jnp.float32),
            pltpu.VMEM((block_rows, 9 * lanes), jnp.bfloat16),
        ],
    )(volume, band, bias)


def run_network(
    em_rows, mask_rows, patch_weight, conv_weight, conv_bias, score_weight, embed_weight
):
    rows_here = em_rows.shape[0]
    side_half = CS // 2
    voxel_count = side_half * side_half * side_half
    channels = conv_weight.shape[2]
    lanes = side_half * channels
    highest = lax.Precision.HIGHEST
    stacked = jnp.concatenate([em_rows[:, None, :], mask_rows], axis=1)
    volume_in = stacked.reshape(rows_here, 3, CS, CS, CS)
    patch_kernel = patch_weight.reshape(channels, 3, 2, 2, 2)
    first_out = lax.conv_general_dilated(
        volume_in,
        patch_kernel,
        (2, 2, 2),
        "VALID",
        dimension_numbers=("NCDHW", "OIDHW", "NDHWC"),
        preferred_element_type=jnp.float32,
    )
    volume = jax.nn.relu(first_out + conv_bias[0]).astype(jnp.bfloat16)
    volume = volume.reshape(rows_here * side_half * side_half, lanes)
    hidden = conv_layers(volume, conv_weight, conv_bias)
    hidden = hidden.reshape(rows_here, side_half * side_half, side_half, channels)
    intersection = mask_rows[:, 0].astype(jnp.float32) * mask_rows[:, 1].astype(jnp.float32)
    intersection = intersection.reshape(rows_here, side_half, 2, side_half, 2, side_half, 2)
    boundary = jnp.mean(intersection, axis=(2, 4, 6))
    boundary = boundary.reshape(rows_here, side_half * side_half, side_half) + 0.1
    pooled = jnp.sum(hidden.astype(jnp.float32) * boundary[..., None], axis=(1, 2))
    pooled = pooled / jnp.sum(boundary, axis=(1, 2))[:, None]
    logits = jnp.dot(pooled, score_weight, precision=highest)
    scores = jax.nn.sigmoid(logits).astype(jnp.bfloat16)
    embedded = jnp.tanh(jnp.dot(pooled, embed_weight.astype(jnp.float32), precision=highest))
    contrib = (scores.astype(jnp.float32)[:, None] * embedded).astype(jnp.bfloat16)
    return (scores, contrib)


def per_device(
    em_cutouts,
    mask_cutouts,
    live_count,
    segment_ids,
    patch_weight,
    conv_weight,
    conv_bias,
    score_weight,
    embed_weight,
):
    bulk_index = lax.axis_index("bulk")
    seg_index = lax.axis_index("seg")
    slots = em_cutouts.shape[2]
    em_local = em_cutouts.reshape(slots, -1)
    mask_local = mask_cutouts.reshape(slots, 2, -1)
    own_count = live_count[bulk_index, seg_index]
    slot_ids = jnp.arange(slots, dtype=jnp.int32)
    live_slot = slot_ids < own_count
    part_score, part_contrib = run_network(
        em_local, mask_local, patch_weight, conv_weight, conv_bias, score_weight, embed_weight
    )
    scores = jnp.where(live_slot, part_score, 0)
    contribs = jnp.where(live_slot[:, None], part_contrib, 0)
    seg_local = jnp.where(live_slot, segment_ids.reshape(slots), -1)
    packed = jnp.concatenate([contribs, seg_local[:, None].astype(jnp.bfloat16)], axis=1)
    gathered = lax.all_gather(packed, "seg", tiled=True)
    all_contrib = gathered[:, :-1]
    all_ids = gathered[:, -1].astype(jnp.int32)
    wanted = seg_index * SEG_DEV + jnp.arange(SEG_DEV, dtype=jnp.int32)
    onehot = (all_ids[None, :] == wanted[:, None]).astype(jnp.bfloat16)
    summed = jnp.dot(onehot, all_contrib, preferred_element_type=jnp.float32)
    return (scores.reshape(1, 1, slots), summed)


def solution(mesh):
    in_specs = (
        P("bulk", "seg", None, None),
        P("bulk", "seg", None, None, None),
        P(),
        P("bulk", "seg", None),
        P(),
        P(),
        P(),
        P(),
        P(),
    )
    out_specs = (P("bulk", "seg", None), P(("bulk", "seg"), None))
    return jax.shard_map(
        per_device, mesh=mesh, in_specs=in_specs, out_specs=out_specs, check_vma=False
    )
```

```python
import jax
import jax.numpy as jnp
from jax import lax
from jax.sharding import PartitionSpec as P
from jax.experimental import pallas as pl
from jax.experimental.pallas import tpu as pltpu

CS = 16
LAYERS = 3
SEG_DEV = 8
BLOCK_PAIRS = 8
PAD_ROWS = 16


def conv_kernel(h_ref, w_ref, b_ref, o_ref, pad_ref, col_ref, band_ref):
    rows, lanes = h_ref.shape
    side = CS // 2
    channels = w_ref.shape[2]
    edge = PAD_ROWS

    @pl.when(pl.program_id(0) == 0)
    def _():
        out_lane = lax.broadcasted_iota(jnp.int32, (channels, lanes), 1)
        in_row = lax.broadcasted_iota(jnp.int32, (channels, lanes), 0)
        spread = (out_lane % channels == in_row).astype(jnp.bfloat16)
        z_lane = out_lane // channels
        for layer_index in range(LAYERS):
            for tap in range(9):
                tiled = [
                    jnp.dot(
                        w_ref[layer_index, tap * 3 + shift_c],
                        spread,
                        preferred_element_type=jnp.float32,
                    )
                    for shift_c in range(3)
                ]
                for z_in in range(side):
                    block = jnp.where(
                        z_lane == z_in + 1,
                        tiled[0],
                        jnp.where(
                            z_lane == z_in,
                            tiled[1],
                            jnp.where(z_lane == z_in - 1, tiled[2], 0.0),
                        ),
                    )
                    start = tap * lanes + z_in * channels
                    band_ref[layer_index, start:start + channels, :] = block.astype(jnp.bfloat16)

    pad_ref[0:edge, :] = jnp.zeros((edge, lanes), jnp.float32)
    pad_ref[edge + rows:, :] = jnp.zeros((edge, lanes), jnp.float32)
    pad_ref[edge:edge + rows, :] = h_ref[...].astype(jnp.float32)
    row_id = lax.broadcasted_iota(jnp.int32, (rows, lanes), 0)
    y_pos = row_id % side
    x_pos = (row_id // side) % side
    for layer_index in range(LAYERS):
        for shift_a in range(3):
            for shift_b in range(3):
                tap = shift_a * 3 + shift_b
                offset = (shift_a - 1) * side + (shift_b - 1)
                window = pad_ref[edge + offset:edge + offset + rows, :]
                x_to = x_pos + (shift_a - 1)
                y_to = y_pos + (shift_b - 1)
                inside = (x_to >= 0) & (x_to < side) & (y_to >= 0) & (y_to < side)
                col_ref[:, tap * lanes:(tap + 1) * lanes] = jnp.where(
                    inside, window, 0.0
                ).astype(jnp.bfloat16)
        summed = jnp.dot(col_ref[...], band_ref[layer_index], preferred_element_type=jnp.float32)
        hidden = jnp.maximum(summed + b_ref[layer_index], 0.0).astype(jnp.bfloat16)
        if layer_index + 1 < LAYERS:
            pad_ref[edge:edge + rows, :] = hidden.astype(jnp.float32)
        else:
            o_ref[...] = hidden


def conv_layers(volume, conv_weight, conv_bias):
    total_rows, lanes = volume.shape
    side = CS // 2
    channels = conv_weight.shape[2]
    taps = conv_weight.transpose(0, 1, 3, 2)
    bias = jnp.tile(conv_bias[1:], (1, side)).reshape(LAYERS, 1, lanes)
    block_rows = BLOCK_PAIRS * side * side
    return pl.pallas_call(
        conv_kernel,
        grid=(total_rows // block_rows,),
        in_specs=[
            pl.BlockSpec((block_rows, lanes), lambda i: (i, 0)),
            pl.BlockSpec((LAYERS, 27, channels, channels), lambda i: (0, 0, 0, 0)),
            pl.BlockSpec((LAYERS, 1, lanes), lambda i: (0, 0, 0)),
        ],
        out_specs=pl.BlockSpec((block_rows, lanes), lambda i: (i, 0)),
        out_shape=jax.ShapeDtypeStruct((total_rows, lanes), jnp.bfloat16),
        scratch_shapes=[
            pltpu.VMEM((block_rows + 2 * PAD_ROWS, lanes), jnp.float32),
            pltpu.VMEM((block_rows, 9 * lanes), jnp.bfloat16),
            pltpu.VMEM((LAYERS, 9 * lanes, lanes), jnp.bfloat16),
        ],
        compiler_params=pltpu.CompilerParams(dimension_semantics=("arbitrary",)),
    )(volume, taps, bias)


def run_network(
    em_rows, mask_rows, patch_weight, conv_weight, conv_bias, score_weight, embed_weight
):
    rows_here = em_rows.shape[0]
    side_half = CS // 2
    voxel_count = side_half * side_half * side_half
    channels = conv_weight.shape[2]
    lanes = side_half * channels
    highest = lax.Precision.HIGHEST
    stacked = jnp.concatenate([em_rows[:, None, :], mask_rows], axis=1)
    volume_in = stacked.reshape(rows_here, 3, CS, CS, CS)
    patch_kernel = patch_weight.reshape(channels, 3, 2, 2, 2)
    first_out = lax.conv_general_dilated(
        volume_in,
        patch_kernel,
        (2, 2, 2),
        "VALID",
        dimension_numbers=("NCDHW", "OIDHW", "NDHWC"),
        preferred_element_type=jnp.float32,
    )
    volume = jax.nn.relu(first_out + conv_bias[0]).astype(jnp.bfloat16)
    volume = volume.reshape(rows_here * side_half * side_half, lanes)
    hidden = conv_layers(volume, conv_weight, conv_bias)
    hidden = hidden.reshape(rows_here, side_half * side_half, side_half, channels)
    intersection = mask_rows[:, 0].astype(jnp.float32) * mask_rows[:, 1].astype(jnp.float32)
    intersection = intersection.reshape(rows_here, side_half, 2, side_half, 2, side_half, 2)
    boundary = jnp.mean(intersection, axis=(2, 4, 6))
    boundary = boundary.reshape(rows_here, side_half * side_half, side_half) + 0.1
    pooled = jnp.sum(hidden.astype(jnp.float32) * boundary[..., None], axis=(1, 2))
    pooled = pooled / jnp.sum(boundary, axis=(1, 2))[:, None]
    logits = jnp.dot(pooled, score_weight, precision=highest)
    scores = jax.nn.sigmoid(logits).astype(jnp.bfloat16)
    embedded = jnp.tanh(jnp.dot(pooled, embed_weight.astype(jnp.float32), precision=highest))
    contrib = (scores.astype(jnp.float32)[:, None] * embedded).astype(jnp.bfloat16)
    return (scores, contrib)


def per_device(
    em_cutouts,
    mask_cutouts,
    live_count,
    segment_ids,
    patch_weight,
    conv_weight,
    conv_bias,
    score_weight,
    embed_weight,
):
    bulk_index = lax.axis_index("bulk")
    seg_index = lax.axis_index("seg")
    slots = em_cutouts.shape[2]
    em_local = em_cutouts.reshape(slots, -1)
    mask_local = mask_cutouts.reshape(slots, 2, -1)
    own_count = live_count[bulk_index, seg_index]
    slot_ids = jnp.arange(slots, dtype=jnp.int32)
    live_slot = slot_ids < own_count
    part_score, part_contrib = run_network(
        em_local, mask_local, patch_weight, conv_weight, conv_bias, score_weight, embed_weight
    )
    scores = jnp.where(live_slot, part_score, 0)
    contribs = jnp.where(live_slot[:, None], part_contrib, 0)
    seg_local = jnp.where(live_slot, segment_ids.reshape(slots), -1)
    packed = jnp.concatenate([contribs, seg_local[:, None].astype(jnp.bfloat16)], axis=1)
    gathered = lax.all_gather(packed, "seg", tiled=True)
    all_contrib = gathered[:, :-1]
    all_ids = gathered[:, -1].astype(jnp.int32)
    wanted = seg_index * SEG_DEV + jnp.arange(SEG_DEV, dtype=jnp.int32)
    onehot = (all_ids[None, :] == wanted[:, None]).astype(jnp.bfloat16)
    summed = jnp.dot(onehot, all_contrib, preferred_element_type=jnp.float32)
    return (scores.reshape(1, 1, slots), summed)


def solution(mesh):
    in_specs = (
        P("bulk", "seg", None, None),
        P("bulk", "seg", None, None, None),
        P(),
        P("bulk", "seg", None),
        P(),
        P(),
        P(),
        P(),
        P(),
    )
    out_specs = (P("bulk", "seg", None), P(("bulk", "seg"), None))
    return jax.shard_map(
        per_device, mesh=mesh, in_specs=in_specs, out_specs=out_specs, check_vma=False
    )
```

```python
import jax
import jax.numpy as jnp
from jax import lax
from jax.sharding import PartitionSpec as P
from jax.experimental import pallas as pl
from jax.experimental.pallas import tpu as pltpu

CS = 16
LAYERS = 3
SEG_DEV = 8
BLOCK_PAIRS = 8
PAD_ROWS = 16


def conv_kernel(x_ref, q_ref, first_bias_ref, w_ref, b_ref, o_ref, pad_ref, col_ref, band_ref):
    rows, lanes = o_ref.shape
    side = CS // 2
    channels = w_ref.shape[2]
    edge = PAD_ROWS

    @pl.when(pl.program_id(0) == 0)
    def _():
        out_lane = lax.broadcasted_iota(jnp.int32, (channels, lanes), 1)
        in_row = lax.broadcasted_iota(jnp.int32, (channels, lanes), 0)
        spread = (out_lane % channels == in_row).astype(jnp.bfloat16)
        z_lane = out_lane // channels
        for layer_index in range(LAYERS):
            for tap in range(9):
                tiled = [
                    jnp.dot(
                        w_ref[layer_index, tap * 3 + shift_c],
                        spread,
                        preferred_element_type=jnp.float32,
                    )
                    for shift_c in range(3)
                ]
                for z_in in range(side):
                    block = jnp.where(
                        z_lane == z_in + 1,
                        tiled[0],
                        jnp.where(
                            z_lane == z_in,
                            tiled[1],
                            jnp.where(z_lane == z_in - 1, tiled[2], 0.0),
                        ),
                    )
                    start = tap * lanes + z_in * channels
                    band_ref[layer_index, start:start + channels, :] = block.astype(jnp.bfloat16)

    pad_ref[0:edge, :] = jnp.zeros((edge, lanes), jnp.float32)
    pad_ref[edge + rows:, :] = jnp.zeros((edge, lanes), jnp.float32)
    first = jnp.dot(x_ref[...], q_ref[...], preferred_element_type=jnp.float32)
    first = jnp.maximum(first + first_bias_ref[...], 0.0).astype(jnp.bfloat16)
    pad_ref[edge:edge + rows, :] = first.astype(jnp.float32)
    row_id = lax.broadcasted_iota(jnp.int32, (rows, lanes), 0)
    y_pos = row_id % side
    x_pos = (row_id // side) % side
    for layer_index in range(LAYERS):
        for shift_a in range(3):
            for shift_b in range(3):
                tap = shift_a * 3 + shift_b
                offset = (shift_a - 1) * side + (shift_b - 1)
                window = pad_ref[edge + offset:edge + offset + rows, :]
                x_to = x_pos + (shift_a - 1)
                y_to = y_pos + (shift_b - 1)
                inside = (x_to >= 0) & (x_to < side) & (y_to >= 0) & (y_to < side)
                col_ref[:, tap * lanes:(tap + 1) * lanes] = jnp.where(
                    inside, window, 0.0
                ).astype(jnp.bfloat16)
        summed = jnp.dot(col_ref[...], band_ref[layer_index], preferred_element_type=jnp.float32)
        hidden = jnp.maximum(summed + b_ref[layer_index], 0.0).astype(jnp.bfloat16)
        if layer_index + 1 < LAYERS:
            pad_ref[edge:edge + rows, :] = hidden.astype(jnp.float32)
        else:
            o_ref[...] = hidden


def conv_layers(features, patch_weight, conv_weight, conv_bias):
    total_rows, feature_count = features.shape
    side = CS // 2
    channels = conv_weight.shape[2]
    lanes = side * channels
    per_cell = patch_weight.reshape(channels, 3, 2, 2, 2).transpose(1, 2, 3, 4, 0)
    z_in = jnp.arange(side)[:, None, None, None]
    z_out = jnp.arange(side)[None, None, :, None]
    patch_matrix = jnp.where(
        z_in == z_out, per_cell[:, :, :, None, :, None, :], 0
    ).reshape(feature_count, lanes)
    first_bias = jnp.tile(conv_bias[0], side).reshape(1, lanes)
    taps = conv_weight.transpose(0, 1, 3, 2)
    bias = jnp.tile(conv_bias[1:], (1, side)).reshape(LAYERS, 1, lanes)
    block_rows = BLOCK_PAIRS * side * side
    return pl.pallas_call(
        conv_kernel,
        grid=(total_rows // block_rows,),
        in_specs=[
            pl.BlockSpec((block_rows, feature_count), lambda i: (i, 0)),
            pl.BlockSpec((feature_count, lanes), lambda i: (0, 0)),
            pl.BlockSpec((1, lanes), lambda i: (0, 0)),
            pl.BlockSpec((LAYERS, 27, channels, channels), lambda i: (0, 0, 0, 0)),
            pl.BlockSpec((LAYERS, 1, lanes), lambda i: (0, 0, 0)),
        ],
        out_specs=pl.BlockSpec((block_rows, lanes), lambda i: (i, 0)),
        out_shape=jax.ShapeDtypeStruct((total_rows, lanes), jnp.bfloat16),
        scratch_shapes=[
            pltpu.VMEM((block_rows + 2 * PAD_ROWS, lanes), jnp.float32),
            pltpu.VMEM((block_rows, 9 * lanes), jnp.bfloat16),
            pltpu.VMEM((LAYERS, 9 * lanes, lanes), jnp.bfloat16),
        ],
        compiler_params=pltpu.CompilerParams(dimension_semantics=("arbitrary",)),
    )(features, patch_matrix, first_bias, taps, bias)


def run_network(
    em_rows, mask_rows, patch_weight, conv_weight, conv_bias, score_weight, embed_weight
):
    rows_here = em_rows.shape[0]
    side_half = CS // 2
    voxel_count = side_half * side_half * side_half
    channels = conv_weight.shape[2]
    lanes = side_half * channels
    highest = lax.Precision.HIGHEST
    stacked = jnp.concatenate([em_rows[:, None, :], mask_rows], axis=1)
    cells = stacked.reshape(rows_here, 3, side_half, 2, side_half, 2 * CS)
    features = cells.transpose(0, 2, 4, 1, 3, 5).reshape(rows_here * side_half * side_half, 12 * CS)
    hidden = conv_layers(features, patch_weight, conv_weight, conv_bias)
    hidden = hidden.reshape(rows_here, side_half * side_half, side_half, channels)
    intersection = mask_rows[:, 0].astype(jnp.float32) * mask_rows[:, 1].astype(jnp.float32)
    intersection = intersection.reshape(rows_here, side_half, 2, side_half, 2, side_half, 2)
    boundary = jnp.mean(intersection, axis=(2, 4, 6))
    boundary = boundary.reshape(rows_here, side_half * side_half, side_half) + 0.1
    pooled = jnp.sum(hidden.astype(jnp.float32) * boundary[..., None], axis=(1, 2))
    pooled = pooled / jnp.sum(boundary, axis=(1, 2))[:, None]
    logits = jnp.dot(pooled, score_weight, precision=highest)
    scores = jax.nn.sigmoid(logits).astype(jnp.bfloat16)
    embedded = jnp.tanh(jnp.dot(pooled, embed_weight.astype(jnp.float32), precision=highest))
    contrib = (scores.astype(jnp.float32)[:, None] * embedded).astype(jnp.bfloat16)
    return (scores, contrib)


def per_device(
    em_cutouts,
    mask_cutouts,
    live_count,
    segment_ids,
    patch_weight,
    conv_weight,
    conv_bias,
    score_weight,
    embed_weight,
):
    bulk_index = lax.axis_index("bulk")
    seg_index = lax.axis_index("seg")
    slots = em_cutouts.shape[2]
    em_local = em_cutouts.reshape(slots, -1)
    mask_local = mask_cutouts.reshape(slots, 2, -1)
    own_count = live_count[bulk_index, seg_index]
    slot_ids = jnp.arange(slots, dtype=jnp.int32)
    live_slot = slot_ids < own_count
    part_score, part_contrib = run_network(
        em_local, mask_local, patch_weight, conv_weight, conv_bias, score_weight, embed_weight
    )
    scores = jnp.where(live_slot, part_score, 0)
    contribs = jnp.where(live_slot[:, None], part_contrib, 0)
    seg_local = jnp.where(live_slot, segment_ids.reshape(slots), -1)
    packed = jnp.concatenate([contribs, seg_local[:, None].astype(jnp.bfloat16)], axis=1)
    gathered = lax.all_gather(packed, "seg", tiled=True)
    all_contrib = gathered[:, :-1]
    all_ids = gathered[:, -1].astype(jnp.int32)
    wanted = seg_index * SEG_DEV + jnp.arange(SEG_DEV, dtype=jnp.int32)
    onehot = (all_ids[None, :] == wanted[:, None]).astype(jnp.bfloat16)
    summed = jnp.dot(onehot, all_contrib, preferred_element_type=jnp.float32)
    return (scores.reshape(1, 1, slots), summed)


def solution(mesh):
    in_specs = (
        P("bulk", "seg", None, None),
        P("bulk", "seg", None, None, None),
        P(),
        P("bulk", "seg", None),
        P(),
        P(),
        P(),
        P(),
        P(),
    )
    out_specs = (P("bulk", "seg", None), P(("bulk", "seg"), None))
    return jax.shard_map(
        per_device, mesh=mesh, in_specs=in_specs, out_specs=out_specs, check_vma=False
    )
```

```python
import jax
import jax.numpy as jnp
from jax import lax
from jax.sharding import PartitionSpec as P
from jax.experimental import pallas as pl
from jax.experimental.pallas import tpu as pltpu

CS = 16
LAYERS = 3
SEG_DEV = 8
BLOCK_PAIRS = 8
PAD_ROWS = 16


def conv_kernel(x_ref, q_ref, first_bias_ref, w_ref, b_ref, o_ref, pad_ref, col_ref, band_ref):
    rows, lanes = o_ref.shape
    side = CS // 2
    channels = w_ref.shape[2]
    edge = PAD_ROWS

    @pl.when(pl.program_id(0) == 0)
    def _():
        out_lane = lax.broadcasted_iota(jnp.int32, (channels, lanes), 1)
        in_row = lax.broadcasted_iota(jnp.int32, (channels, lanes), 0)
        spread = (out_lane % channels == in_row).astype(jnp.bfloat16)
        z_lane = out_lane // channels
        for layer_index in range(LAYERS):
            for tap in range(9):
                tiled = [
                    jnp.dot(
                        w_ref[layer_index, tap * 3 + shift_c],
                        spread,
                        preferred_element_type=jnp.float32,
                    )
                    for shift_c in range(3)
                ]
                for z_in in range(side):
                    block = jnp.where(
                        z_lane == z_in + 1,
                        tiled[0],
                        jnp.where(
                            z_lane == z_in,
                            tiled[1],
                            jnp.where(z_lane == z_in - 1, tiled[2], 0.0),
                        ),
                    )
                    start = tap * lanes + z_in * channels
                    band_ref[layer_index, start:start + channels, :] = block.astype(jnp.bfloat16)

    pad_ref[0:edge, :] = jnp.zeros((edge, lanes), jnp.float32)
    pad_ref[edge + rows:, :] = jnp.zeros((edge, lanes), jnp.float32)
    first = jnp.dot(x_ref[...], q_ref[...], preferred_element_type=jnp.float32)
    first = jnp.maximum(first + first_bias_ref[...], 0.0).astype(jnp.bfloat16)
    pad_ref[edge:edge + rows, :] = first.astype(jnp.float32)
    row_id = lax.broadcasted_iota(jnp.int32, (rows, lanes), 0)
    y_pos = row_id % side
    x_pos = (row_id // side) % side
    for layer_index in range(LAYERS):
        for shift_a in range(3):
            for shift_b in range(3):
                tap = shift_a * 3 + shift_b
                offset = (shift_a - 1) * side + (shift_b - 1)
                window = pad_ref[edge + offset:edge + offset + rows, :]
                x_to = x_pos + (shift_a - 1)
                y_to = y_pos + (shift_b - 1)
                inside = (x_to >= 0) & (x_to < side) & (y_to >= 0) & (y_to < side)
                col_ref[:, tap * lanes:(tap + 1) * lanes] = jnp.where(
                    inside, window, 0.0
                ).astype(jnp.bfloat16)
        summed = jnp.dot(col_ref[...], band_ref[layer_index], preferred_element_type=jnp.float32)
        hidden = jnp.maximum(summed + b_ref[layer_index], 0.0).astype(jnp.bfloat16)
        if layer_index + 1 < LAYERS:
            pad_ref[edge:edge + rows, :] = hidden.astype(jnp.float32)
        else:
            o_ref[...] = hidden


def conv_layers(features, patch_weight, conv_weight, conv_bias):
    total_rows, feature_count = features.shape
    side = CS // 2
    channels = conv_weight.shape[2]
    lanes = side * channels
    per_cell = patch_weight.reshape(channels, 3, 2, 2, 2).transpose(1, 2, 3, 4, 0)
    z_in = jnp.arange(side)[:, None, None, None]
    z_out = jnp.arange(side)[None, None, :, None]
    patch_matrix = jnp.where(
        z_in == z_out, per_cell[:, :, :, None, :, None, :], 0
    ).reshape(feature_count, lanes)
    first_bias = jnp.tile(conv_bias[0], side).reshape(1, lanes)
    taps = conv_weight.transpose(0, 1, 3, 2)
    bias = jnp.tile(conv_bias[1:], (1, side)).reshape(LAYERS, 1, lanes)
    block_rows = BLOCK_PAIRS * side * side
    return pl.pallas_call(
        conv_kernel,
        grid=(total_rows // block_rows,),
        in_specs=[
            pl.BlockSpec((block_rows, feature_count), lambda i: (i, 0)),
            pl.BlockSpec((feature_count, lanes), lambda i: (0, 0)),
            pl.BlockSpec((1, lanes), lambda i: (0, 0)),
            pl.BlockSpec((LAYERS, 27, channels, channels), lambda i: (0, 0, 0, 0)),
            pl.BlockSpec((LAYERS, 1, lanes), lambda i: (0, 0, 0)),
        ],
        out_specs=pl.BlockSpec((block_rows, lanes), lambda i: (i, 0)),
        out_shape=jax.ShapeDtypeStruct((total_rows, lanes), jnp.bfloat16),
        scratch_shapes=[
            pltpu.VMEM((block_rows + 2 * PAD_ROWS, lanes), jnp.float32),
            pltpu.VMEM((block_rows, 9 * lanes), jnp.bfloat16),
            pltpu.VMEM((LAYERS, 9 * lanes, lanes), jnp.bfloat16),
        ],
        compiler_params=pltpu.CompilerParams(dimension_semantics=("arbitrary",)),
    )(features, patch_matrix, first_bias, taps, bias)


def run_network(
    em_rows, mask_rows, patch_weight, conv_weight, conv_bias, score_weight, embed_weight
):
    rows_here = em_rows.shape[0]
    side_half = CS // 2
    voxel_count = side_half * side_half * side_half
    channels = conv_weight.shape[2]
    lanes = side_half * channels
    highest = lax.Precision.HIGHEST
    stacked = jnp.concatenate([em_rows[:, None, :], mask_rows], axis=1)
    cells = stacked.reshape(rows_here, 3, side_half, 2, side_half, 2 * CS)
    features = cells.transpose(0, 2, 4, 1, 3, 5).reshape(rows_here * side_half * side_half, 12 * CS)
    hidden = conv_layers(features, patch_weight, conv_weight, conv_bias)
    hidden = hidden.reshape(rows_here, side_half * side_half, side_half, channels)
    intersection = mask_rows[:, 0].astype(jnp.float32) * mask_rows[:, 1].astype(jnp.float32)
    intersection = intersection.reshape(rows_here, side_half, 2, side_half, 2, side_half, 2)
    boundary = jnp.mean(intersection, axis=(2, 4, 6))
    boundary = boundary.reshape(rows_here, side_half * side_half, side_half) + 0.1
    pooled = jnp.sum(hidden.astype(jnp.float32) * boundary[..., None], axis=(1, 2))
    pooled = pooled / jnp.sum(boundary, axis=(1, 2))[:, None]
    logits = jnp.dot(pooled, score_weight, precision=highest)
    scores = jax.nn.sigmoid(logits).astype(jnp.bfloat16)
    embedded = jnp.tanh(jnp.dot(pooled, embed_weight.astype(jnp.float32), precision=highest))
    contrib = (scores.astype(jnp.float32)[:, None] * embedded).astype(jnp.bfloat16)
    return (scores, contrib)


def per_device(
    em_cutouts,
    mask_cutouts,
    live_count,
    segment_ids,
    patch_weight,
    conv_weight,
    conv_bias,
    score_weight,
    embed_weight,
):
    bulk_index = lax.axis_index("bulk")
    seg_index = lax.axis_index("seg")
    slots = em_cutouts.shape[2]
    em_local = em_cutouts.reshape(slots, -1)
    mask_local = mask_cutouts.reshape(slots, 2, -1)
    own_count = live_count[bulk_index, seg_index]
    slot_ids = jnp.arange(slots, dtype=jnp.int32)
    live_slot = slot_ids < own_count
    part_score, part_contrib = run_network(
        em_local, mask_local, patch_weight, conv_weight, conv_bias, score_weight, embed_weight
    )
    scores = jnp.where(live_slot, part_score, 0)
    contribs = jnp.where(live_slot[:, None], part_contrib, 0)
    n_seg = lax.axis_size("seg")
    seg_local = jnp.where(live_slot, segment_ids.reshape(slots), -1)
    segment_row = jnp.arange(n_seg * SEG_DEV, dtype=jnp.int32)
    onehot = (segment_row[:, None] == seg_local[None, :]).astype(jnp.bfloat16)
    partial_value = jnp.dot(onehot, contribs, preferred_element_type=jnp.float32)
    partial_value = partial_value.reshape(n_seg, SEG_DEV, -1)
    arrived = lax.all_to_all(partial_value, "seg", 0, 0, tiled=True)
    summed = jnp.sum(arrived, axis=0)
    return (scores.reshape(1, 1, slots), summed)


def solution(mesh):
    in_specs = (
        P("bulk", "seg", None, None),
        P("bulk", "seg", None, None, None),
        P(),
        P("bulk", "seg", None),
        P(),
        P(),
        P(),
        P(),
        P(),
    )
    out_specs = (P("bulk", "seg", None), P(("bulk", "seg"), None))
    return jax.shard_map(
        per_device, mesh=mesh, in_specs=in_specs, out_specs=out_specs, check_vma=False
    )
```

```python
import jax
import jax.numpy as jnp
from jax import lax
from jax.sharding import PartitionSpec as P
from jax.experimental import pallas as pl
from jax.experimental.pallas import tpu as pltpu

CS = 16
LAYERS = 3
SEG_DEV = 8
BLOCK_PAIRS = 8
PAD_ROWS = 16


def conv_kernel(
    x_ref, q_ref, first_bias_ref, w_ref, b_ref, pool_ref, weight_ref, pad_ref, col_ref, band_ref
):
    rows, lanes = pad_ref.shape[0] - 2 * PAD_ROWS, pad_ref.shape[1]
    side = CS // 2
    channels = w_ref.shape[2]
    edge = PAD_ROWS

    @pl.when(pl.program_id(0) == 0)
    def _():
        out_lane = lax.broadcasted_iota(jnp.int32, (channels, lanes), 1)
        in_row = lax.broadcasted_iota(jnp.int32, (channels, lanes), 0)
        spread = (out_lane % channels == in_row).astype(jnp.bfloat16)
        z_lane = out_lane // channels
        for layer_index in range(LAYERS):
            for tap in range(9):
                tiled = [
                    jnp.dot(
                        w_ref[layer_index, tap * 3 + shift_c],
                        spread,
                        preferred_element_type=jnp.float32,
                    )
                    for shift_c in range(3)
                ]
                for z_in in range(side):
                    block = jnp.where(
                        z_lane == z_in + 1,
                        tiled[0],
                        jnp.where(
                            z_lane == z_in,
                            tiled[1],
                            jnp.where(z_lane == z_in - 1, tiled[2], 0.0),
                        ),
                    )
                    start = tap * lanes + z_in * channels
                    band_ref[layer_index, start:start + channels, :] = block.astype(jnp.bfloat16)

    pad_ref[0:edge, :] = jnp.zeros((edge, lanes), jnp.float32)
    pad_ref[edge + rows:, :] = jnp.zeros((edge, lanes), jnp.float32)
    first = jnp.dot(x_ref[...], q_ref[...], preferred_element_type=jnp.float32)
    first = jnp.maximum(first + first_bias_ref[...], 0.0).astype(jnp.bfloat16)
    pad_ref[edge:edge + rows, :] = first.astype(jnp.float32)
    row_id = lax.broadcasted_iota(jnp.int32, (rows, lanes), 0)
    y_pos = row_id % side
    x_pos = (row_id // side) % side
    for layer_index in range(LAYERS):
        for shift_a in range(3):
            for shift_b in range(3):
                tap = shift_a * 3 + shift_b
                offset = (shift_a - 1) * side + (shift_b - 1)
                window = pad_ref[edge + offset:edge + offset + rows, :]
                x_to = x_pos + (shift_a - 1)
                y_to = y_pos + (shift_b - 1)
                inside = (x_to >= 0) & (x_to < side) & (y_to >= 0) & (y_to < side)
                col_ref[:, tap * lanes:(tap + 1) * lanes] = jnp.where(
                    inside, window, 0.0
                ).astype(jnp.bfloat16)
        summed = jnp.dot(col_ref[...], band_ref[layer_index], preferred_element_type=jnp.float32)
        hidden = jnp.maximum(summed + b_ref[layer_index], 0.0).astype(jnp.bfloat16)
        pad_ref[edge:edge + rows, :] = hidden.astype(jnp.float32)
    masks = x_ref[:, 0:128].astype(jnp.float32)
    overlap = masks * pltpu.roll(masks, 64, 1)
    over_hi = overlap.astype(jnp.bfloat16)
    over_lo = (overlap - over_hi.astype(jnp.float32)).astype(jnp.bfloat16)
    cell = lax.broadcasted_iota(jnp.int32, (128, lanes), 0)
    z_of_lane = lax.broadcasted_iota(jnp.int32, (128, lanes), 1) // channels
    gather = ((cell < 64) & ((cell // 2) % side == z_of_lane)).astype(jnp.bfloat16)
    cell_sum = jnp.dot(over_hi, gather, preferred_element_type=jnp.float32) + jnp.dot(
        over_lo, gather, preferred_element_type=jnp.float32
    )
    boundary = cell_sum * 0.125 + 0.1
    final = pad_ref[edge:edge + rows, :]
    pairs = rows // (side * side)
    pool_ref[...] = jnp.sum((final * boundary).reshape(pairs, side * side, lanes), axis=1)
    weight_ref[...] = jnp.sum(boundary.reshape(pairs, side * side, lanes), axis=1)


def conv_layers(features, patch_weight, conv_weight, conv_bias):
    total_rows, feature_count = features.shape
    side = CS // 2
    channels = conv_weight.shape[2]
    lanes = side * channels
    per_cell = patch_weight.reshape(channels, 3, 2, 2, 2).transpose(1, 2, 3, 4, 0)[
        jnp.array([1, 2, 0])
    ]
    z_in = jnp.arange(side)[:, None, None, None]
    z_out = jnp.arange(side)[None, None, :, None]
    patch_matrix = jnp.where(
        z_in == z_out, per_cell[:, :, :, None, :, None, :], 0
    ).reshape(feature_count, lanes)
    first_bias = jnp.tile(conv_bias[0], side).reshape(1, lanes)
    taps = conv_weight.transpose(0, 1, 3, 2)
    bias = jnp.tile(conv_bias[1:], (1, side)).reshape(LAYERS, 1, lanes)
    block_rows = BLOCK_PAIRS * side * side
    return pl.pallas_call(
        conv_kernel,
        grid=(total_rows // block_rows,),
        in_specs=[
            pl.BlockSpec((block_rows, feature_count), lambda i: (i, 0)),
            pl.BlockSpec((feature_count, lanes), lambda i: (0, 0)),
            pl.BlockSpec((1, lanes), lambda i: (0, 0)),
            pl.BlockSpec((LAYERS, 27, channels, channels), lambda i: (0, 0, 0, 0)),
            pl.BlockSpec((LAYERS, 1, lanes), lambda i: (0, 0, 0)),
        ],
        out_specs=[
            pl.BlockSpec((BLOCK_PAIRS, lanes), lambda i: (i, 0)),
            pl.BlockSpec((BLOCK_PAIRS, lanes), lambda i: (i, 0)),
        ],
        out_shape=[
            jax.ShapeDtypeStruct((total_rows // (side * side), lanes), jnp.float32),
            jax.ShapeDtypeStruct((total_rows // (side * side), lanes), jnp.float32),
        ],
        scratch_shapes=[
            pltpu.VMEM((block_rows + 2 * PAD_ROWS, lanes), jnp.float32),
            pltpu.VMEM((block_rows, 9 * lanes), jnp.bfloat16),
            pltpu.VMEM((LAYERS, 9 * lanes, lanes), jnp.bfloat16),
        ],
        compiler_params=pltpu.CompilerParams(dimension_semantics=("arbitrary",)),
    )(features, patch_matrix, first_bias, taps, bias)


def run_network(
    em_rows, mask_rows, patch_weight, conv_weight, conv_bias, score_weight, embed_weight
):
    rows_here = em_rows.shape[0]
    side_half = CS // 2
    voxel_count = side_half * side_half * side_half
    channels = conv_weight.shape[2]
    lanes = side_half * channels
    highest = lax.Precision.HIGHEST
    stacked = jnp.concatenate([mask_rows, em_rows[:, None, :]], axis=1)
    cells = stacked.reshape(rows_here, 3, side_half, 2, side_half, 2 * CS)
    features = cells.transpose(0, 2, 4, 1, 3, 5).reshape(rows_here * side_half * side_half, 12 * CS)
    pool_sum, weight_sum = conv_layers(features, patch_weight, conv_weight, conv_bias)
    pooled = jnp.sum(pool_sum.reshape(rows_here, side_half, channels), axis=1)
    total_weight = jnp.sum(weight_sum.reshape(rows_here, side_half, channels)[:, :, 0], axis=1)
    pooled = pooled / total_weight[:, None]
    logits = jnp.dot(pooled, score_weight, precision=highest)
    scores = jax.nn.sigmoid(logits).astype(jnp.bfloat16)
    embedded = jnp.tanh(jnp.dot(pooled, embed_weight.astype(jnp.float32), precision=highest))
    contrib = (scores.astype(jnp.float32)[:, None] * embedded).astype(jnp.bfloat16)
    return (scores, contrib)


def per_device(
    em_cutouts,
    mask_cutouts,
    live_count,
    segment_ids,
    patch_weight,
    conv_weight,
    conv_bias,
    score_weight,
    embed_weight,
):
    bulk_index = lax.axis_index("bulk")
    seg_index = lax.axis_index("seg")
    slots = em_cutouts.shape[2]
    em_local = em_cutouts.reshape(slots, -1)
    mask_local = mask_cutouts.reshape(slots, 2, -1)
    own_count = live_count[bulk_index, seg_index]
    slot_ids = jnp.arange(slots, dtype=jnp.int32)
    live_slot = slot_ids < own_count
    part_score, part_contrib = run_network(
        em_local, mask_local, patch_weight, conv_weight, conv_bias, score_weight, embed_weight
    )
    scores = jnp.where(live_slot, part_score, 0)
    contribs = jnp.where(live_slot[:, None], part_contrib, 0)
    n_seg = lax.axis_size("seg")
    seg_local = jnp.where(live_slot, segment_ids.reshape(slots), -1)
    segment_row = jnp.arange(n_seg * SEG_DEV, dtype=jnp.int32)
    onehot = (segment_row[:, None] == seg_local[None, :]).astype(jnp.bfloat16)
    partial_value = jnp.dot(onehot, contribs, preferred_element_type=jnp.float32)
    partial_value = partial_value.reshape(n_seg, SEG_DEV, -1)
    arrived = lax.all_to_all(partial_value, "seg", 0, 0, tiled=True)
    summed = jnp.sum(arrived, axis=0)
    return (scores.reshape(1, 1, slots), summed)


def solution(mesh):
    in_specs = (
        P("bulk", "seg", None, None),
        P("bulk", "seg", None, None, None),
        P(),
        P("bulk", "seg", None),
        P(),
        P(),
        P(),
        P(),
        P(),
    )
    out_specs = (P("bulk", "seg", None), P(("bulk", "seg"), None))
    return jax.shard_map(
        per_device, mesh=mesh, in_specs=in_specs, out_specs=out_specs, check_vma=False
    )
```

```python
import jax
import jax.numpy as jnp
from jax import lax
from jax.sharding import PartitionSpec as P
from jax.experimental import pallas as pl
from jax.experimental.pallas import tpu as pltpu

CS = 16
LAYERS = 3
SEG_DEV = 8
BLOCK_PAIRS = 8
PAD_ROWS = 16


def conv_kernel(
    x_ref, q_ref, first_bias_ref, w_ref, b_ref, pool_ref, weight_ref, pad_ref, col_ref, band_ref
):
    rows, lanes = pad_ref.shape[0] - 2 * PAD_ROWS, pad_ref.shape[1]
    side = CS // 2
    channels = w_ref.shape[2]
    edge = PAD_ROWS

    @pl.when(pl.program_id(0) == 0)
    def _():
        out_lane = lax.broadcasted_iota(jnp.int32, (channels, lanes), 1)
        in_row = lax.broadcasted_iota(jnp.int32, (channels, lanes), 0)
        spread = (out_lane % channels == in_row).astype(jnp.bfloat16)
        z_lane = out_lane // channels
        for layer_index in range(LAYERS):
            for tap in range(9):
                tiled = [
                    jnp.dot(
                        w_ref[layer_index, tap * 3 + shift_c],
                        spread,
                        preferred_element_type=jnp.float32,
                    )
                    for shift_c in range(3)
                ]
                for z_in in range(side):
                    block = jnp.where(
                        z_lane == z_in + 1,
                        tiled[0],
                        jnp.where(
                            z_lane == z_in,
                            tiled[1],
                            jnp.where(z_lane == z_in - 1, tiled[2], 0.0),
                        ),
                    )
                    start = tap * lanes + z_in * channels
                    band_ref[layer_index, start:start + channels, :] = block.astype(jnp.bfloat16)

    pad_ref[0:edge, :] = jnp.zeros((edge, lanes), jnp.float32)
    pad_ref[edge + rows:, :] = jnp.zeros((edge, lanes), jnp.float32)
    first = jnp.dot(x_ref[...], q_ref[...], preferred_element_type=jnp.float32)
    first = jnp.maximum(first + first_bias_ref[...], 0.0).astype(jnp.bfloat16)
    pad_ref[edge:edge + rows, :] = first.astype(jnp.float32)
    row_id = lax.broadcasted_iota(jnp.int32, (rows, lanes), 0)
    y_pos = row_id % side
    x_pos = (row_id // side) % side
    for layer_index in range(LAYERS):
        for shift_a in range(3):
            for shift_b in range(3):
                tap = shift_a * 3 + shift_b
                offset = (shift_a - 1) * side + (shift_b - 1)
                window = pad_ref[edge + offset:edge + offset + rows, :]
                x_to = x_pos + (shift_a - 1)
                y_to = y_pos + (shift_b - 1)
                inside = (x_to >= 0) & (x_to < side) & (y_to >= 0) & (y_to < side)
                col_ref[:, tap * lanes:(tap + 1) * lanes] = jnp.where(
                    inside, window, 0.0
                ).astype(jnp.bfloat16)
        summed = jnp.dot(col_ref[...], band_ref[layer_index], preferred_element_type=jnp.float32)
        hidden = jnp.maximum(summed + b_ref[layer_index], 0.0).astype(jnp.bfloat16)
        pad_ref[edge:edge + rows, :] = hidden.astype(jnp.float32)
    masks = x_ref[:, 0:128].astype(jnp.float32)
    overlap = masks * pltpu.roll(masks, 64, 1)
    over_hi = overlap.astype(jnp.bfloat16)
    over_lo = (overlap - over_hi.astype(jnp.float32)).astype(jnp.bfloat16)
    cell = lax.broadcasted_iota(jnp.int32, (128, lanes), 0)
    z_of_lane = lax.broadcasted_iota(jnp.int32, (128, lanes), 1) // channels
    gather = ((cell < 64) & ((cell // 2) % side == z_of_lane)).astype(jnp.bfloat16)
    cell_sum = jnp.dot(over_hi, gather, preferred_element_type=jnp.float32) + jnp.dot(
        over_lo, gather, preferred_element_type=jnp.float32
    )
    boundary = cell_sum * 0.125 + 0.1
    final = pad_ref[edge:edge + rows, :]
    pairs = rows // (side * side)
    pool_ref[...] = jnp.sum((final * boundary).reshape(pairs, side * side, lanes), axis=1)
    weight_ref[...] = jnp.sum(boundary.reshape(pairs, side * side, lanes), axis=1)


def conv_layers(features, patch_weight, conv_weight, conv_bias):
    total_rows, feature_count = features.shape
    side = CS // 2
    channels = conv_weight.shape[2]
    lanes = side * channels
    per_cell = patch_weight.reshape(channels, 3, 2, 2, 2).transpose(1, 2, 3, 4, 0)[
        jnp.array([1, 2, 0])
    ]
    z_in = jnp.arange(side)[:, None, None, None]
    z_out = jnp.arange(side)[None, None, :, None]
    patch_matrix = jnp.where(
        z_in == z_out, per_cell[:, :, :, None, :, None, :], 0
    ).reshape(feature_count, lanes)
    first_bias = jnp.tile(conv_bias[0], side).reshape(1, lanes)
    taps = conv_weight.transpose(0, 1, 3, 2)
    bias = jnp.tile(conv_bias[1:], (1, side)).reshape(LAYERS, 1, lanes)
    block_rows = BLOCK_PAIRS * side * side
    return pl.pallas_call(
        conv_kernel,
        grid=(total_rows // block_rows,),
        in_specs=[
            pl.BlockSpec((block_rows, feature_count), lambda i: (i, 0)),
            pl.BlockSpec((feature_count, lanes), lambda i: (0, 0)),
            pl.BlockSpec((1, lanes), lambda i: (0, 0)),
            pl.BlockSpec((LAYERS, 27, channels, channels), lambda i: (0, 0, 0, 0)),
            pl.BlockSpec((LAYERS, 1, lanes), lambda i: (0, 0, 0)),
        ],
        out_specs=[
            pl.BlockSpec((BLOCK_PAIRS, lanes), lambda i: (i, 0)),
            pl.BlockSpec((BLOCK_PAIRS, lanes), lambda i: (i, 0)),
        ],
        out_shape=[
            jax.ShapeDtypeStruct((total_rows // (side * side), lanes), jnp.float32),
            jax.ShapeDtypeStruct((total_rows // (side * side), lanes), jnp.float32),
        ],
        scratch_shapes=[
            pltpu.VMEM((block_rows + 2 * PAD_ROWS, lanes), jnp.float32),
            pltpu.VMEM((block_rows, 9 * lanes), jnp.bfloat16),
            pltpu.VMEM((LAYERS, 9 * lanes, lanes), jnp.bfloat16),
        ],
        compiler_params=pltpu.CompilerParams(dimension_semantics=("arbitrary",)),
    )(features, patch_matrix, first_bias, taps, bias)


def run_network(
    em_rows, mask_rows, patch_weight, conv_weight, conv_bias, score_weight, embed_weight
):
    rows_here = em_rows.shape[0]
    side_half = CS // 2
    voxel_count = side_half * side_half * side_half
    channels = conv_weight.shape[2]
    lanes = side_half * channels
    highest = lax.Precision.HIGHEST
    stacked = jnp.concatenate([mask_rows, em_rows[:, None, :]], axis=1)
    cells = stacked.reshape(rows_here, 3, side_half, 2, side_half, 2 * CS)
    features = jnp.concatenate(
        [
            cells[:, channel, :, half].reshape(rows_here * side_half * side_half, 2 * CS)
            for channel in range(3)
            for half in range(2)
        ],
        axis=1,
    )
    pool_sum, weight_sum = conv_layers(features, patch_weight, conv_weight, conv_bias)
    pooled = jnp.sum(pool_sum.reshape(rows_here, side_half, channels), axis=1)
    total_weight = jnp.sum(weight_sum.reshape(rows_here, side_half, channels)[:, :, 0], axis=1)
    pooled = pooled / total_weight[:, None]
    logits = jnp.dot(pooled, score_weight, precision=highest)
    scores = jax.nn.sigmoid(logits).astype(jnp.bfloat16)
    embedded = jnp.tanh(jnp.dot(pooled, embed_weight.astype(jnp.float32), precision=highest))
    contrib = (scores.astype(jnp.float32)[:, None] * embedded).astype(jnp.bfloat16)
    return (scores, contrib)


def per_device(
    em_cutouts,
    mask_cutouts,
    live_count,
    segment_ids,
    patch_weight,
    conv_weight,
    conv_bias,
    score_weight,
    embed_weight,
):
    bulk_index = lax.axis_index("bulk")
    seg_index = lax.axis_index("seg")
    slots = em_cutouts.shape[2]
    em_local = em_cutouts.reshape(slots, -1)
    mask_local = mask_cutouts.reshape(slots, 2, -1)
    own_count = live_count[bulk_index, seg_index]
    slot_ids = jnp.arange(slots, dtype=jnp.int32)
    live_slot = slot_ids < own_count
    part_score, part_contrib = run_network(
        em_local, mask_local, patch_weight, conv_weight, conv_bias, score_weight, embed_weight
    )
    scores = jnp.where(live_slot, part_score, 0)
    contribs = jnp.where(live_slot[:, None], part_contrib, 0)
    n_seg = lax.axis_size("seg")
    seg_local = jnp.where(live_slot, segment_ids.reshape(slots), -1)
    segment_row = jnp.arange(n_seg * SEG_DEV, dtype=jnp.int32)
    onehot = (segment_row[:, None] == seg_local[None, :]).astype(jnp.bfloat16)
    partial_value = jnp.dot(onehot, contribs, preferred_element_type=jnp.float32)
    partial_value = partial_value.reshape(n_seg, SEG_DEV, -1)
    arrived = lax.all_to_all(partial_value, "seg", 0, 0, tiled=True)
    summed = jnp.sum(arrived, axis=0)
    return (scores.reshape(1, 1, slots), summed)


def solution(mesh):
    in_specs = (
        P("bulk", "seg", None, None),
        P("bulk", "seg", None, None, None),
        P(),
        P("bulk", "seg", None),
        P(),
        P(),
        P(),
        P(),
        P(),
    )
    out_specs = (P("bulk", "seg", None), P(("bulk", "seg"), None))
    return jax.shard_map(
        per_device, mesh=mesh, in_specs=in_specs, out_specs=out_specs, check_vma=False
    )
```

```python
import jax
import jax.numpy as jnp
from jax import lax
from jax.sharding import PartitionSpec as P
from jax.experimental import pallas as pl
from jax.experimental.pallas import tpu as pltpu

CS = 16
LAYERS = 3
SEG_DEV = 8
BLOCK_PAIRS = 8
PAD_ROWS = 16


def conv_kernel(
    x_ref, q_ref, first_bias_ref, w_ref, b_ref, pool_ref, weight_ref, pad_ref, col_ref, band_ref
):
    rows, lanes = pad_ref.shape[0] - 2 * PAD_ROWS, pad_ref.shape[1]
    side = CS // 2
    channels = w_ref.shape[2]
    edge = PAD_ROWS

    @pl.when(pl.program_id(0) == 0)
    def _():
        out_lane = lax.broadcasted_iota(jnp.int32, (channels, lanes), 1)
        in_row = lax.broadcasted_iota(jnp.int32, (channels, lanes), 0)
        spread = (out_lane % channels == in_row).astype(jnp.bfloat16)
        z_lane = out_lane // channels
        for layer_index in range(LAYERS):
            for tap in range(9):
                tiled = [
                    jnp.dot(
                        w_ref[layer_index, tap * 3 + shift_c],
                        spread,
                        preferred_element_type=jnp.float32,
                    )
                    for shift_c in range(3)
                ]
                for z_in in range(side):
                    block = jnp.where(
                        z_lane == z_in + 1,
                        tiled[0],
                        jnp.where(
                            z_lane == z_in,
                            tiled[1],
                            jnp.where(z_lane == z_in - 1, tiled[2], 0.0),
                        ),
                    )
                    start = tap * lanes + z_in * channels
                    band_ref[layer_index, start:start + channels, :] = block.astype(jnp.bfloat16)

    pad_ref[0:edge, :] = jnp.zeros((edge, lanes), jnp.float32)
    pad_ref[edge + rows:, :] = jnp.zeros((edge, lanes), jnp.float32)
    first = jnp.dot(x_ref[...], q_ref[...], preferred_element_type=jnp.float32)
    first = jnp.maximum(first + first_bias_ref[...], 0.0).astype(jnp.bfloat16)
    pad_ref[edge:edge + rows, :] = first.astype(jnp.float32)
    row_id = lax.broadcasted_iota(jnp.int32, (rows, 1), 0)
    y_pos = row_id % side
    x_pos = (row_id // side) % side
    for layer_index in range(LAYERS):
        for shift_a in range(3):
            for shift_b in range(3):
                tap = shift_a * 3 + shift_b
                offset = (shift_a - 1) * side + (shift_b - 1)
                window = pad_ref[edge + offset:edge + offset + rows, :]
                x_to = x_pos + (shift_a - 1)
                y_to = y_pos + (shift_b - 1)
                inside = (x_to >= 0) & (x_to < side) & (y_to >= 0) & (y_to < side)
                col_ref[:, tap * lanes:(tap + 1) * lanes] = jnp.where(
                    inside, window, 0.0
                ).astype(jnp.bfloat16)
        summed = jnp.dot(col_ref[...], band_ref[layer_index], preferred_element_type=jnp.float32)
        hidden = jnp.maximum(summed + b_ref[layer_index], 0.0).astype(jnp.bfloat16)
        pad_ref[edge:edge + rows, :] = hidden.astype(jnp.float32)
    masks = x_ref[:, 0:128].astype(jnp.float32)
    overlap = masks * pltpu.roll(masks, 64, 1)
    over_hi = overlap.astype(jnp.bfloat16)
    over_lo = (overlap - over_hi.astype(jnp.float32)).astype(jnp.bfloat16)
    cell = lax.broadcasted_iota(jnp.int32, (128, lanes), 0)
    z_of_lane = lax.broadcasted_iota(jnp.int32, (128, lanes), 1) // channels
    gather = ((cell < 64) & ((cell // 2) % side == z_of_lane)).astype(jnp.bfloat16)
    cell_sum = jnp.dot(over_hi, gather, preferred_element_type=jnp.float32) + jnp.dot(
        over_lo, gather, preferred_element_type=jnp.float32
    )
    boundary = cell_sum * 0.125 + 0.1
    final = pad_ref[edge:edge + rows, :]
    pairs = rows // (side * side)
    pool_ref[...] = jnp.sum((final * boundary).reshape(pairs, side * side, lanes), axis=1)
    weight_ref[...] = jnp.sum(boundary.reshape(pairs, side * side, lanes), axis=1)


def conv_layers(features, patch_weight, conv_weight, conv_bias):
    total_rows, feature_count = features.shape
    side = CS // 2
    channels = conv_weight.shape[2]
    lanes = side * channels
    per_cell = patch_weight.reshape(channels, 3, 2, 2, 2).transpose(1, 2, 3, 4, 0)[
        jnp.array([1, 2, 0])
    ]
    z_in = jnp.arange(side)[:, None, None, None]
    z_out = jnp.arange(side)[None, None, :, None]
    patch_matrix = jnp.where(
        z_in == z_out, per_cell[:, :, :, None, :, None, :], 0
    ).reshape(feature_count, lanes)
    first_bias = jnp.tile(conv_bias[0], side).reshape(1, lanes)
    taps = conv_weight.transpose(0, 1, 3, 2)
    bias = jnp.tile(conv_bias[1:], (1, side)).reshape(LAYERS, 1, lanes)
    block_rows = BLOCK_PAIRS * side * side
    return pl.pallas_call(
        conv_kernel,
        grid=(total_rows // block_rows,),
        in_specs=[
            pl.BlockSpec((block_rows, feature_count), lambda i: (i, 0)),
            pl.BlockSpec((feature_count, lanes), lambda i: (0, 0)),
            pl.BlockSpec((1, lanes), lambda i: (0, 0)),
            pl.BlockSpec((LAYERS, 27, channels, channels), lambda i: (0, 0, 0, 0)),
            pl.BlockSpec((LAYERS, 1, lanes), lambda i: (0, 0, 0)),
        ],
        out_specs=[
            pl.BlockSpec((BLOCK_PAIRS, lanes), lambda i: (i, 0)),
            pl.BlockSpec((BLOCK_PAIRS, lanes), lambda i: (i, 0)),
        ],
        out_shape=[
            jax.ShapeDtypeStruct((total_rows // (side * side), lanes), jnp.float32),
            jax.ShapeDtypeStruct((total_rows // (side * side), lanes), jnp.float32),
        ],
        scratch_shapes=[
            pltpu.VMEM((block_rows + 2 * PAD_ROWS, lanes), jnp.float32),
            pltpu.VMEM((block_rows, 9 * lanes), jnp.bfloat16),
            pltpu.VMEM((LAYERS, 9 * lanes, lanes), jnp.bfloat16),
        ],
        compiler_params=pltpu.CompilerParams(dimension_semantics=("arbitrary",)),
    )(features, patch_matrix, first_bias, taps, bias)


def run_network(
    em_rows, mask_rows, patch_weight, conv_weight, conv_bias, score_weight, embed_weight
):
    rows_here = em_rows.shape[0]
    side_half = CS // 2
    voxel_count = side_half * side_half * side_half
    channels = conv_weight.shape[2]
    lanes = side_half * channels
    highest = lax.Precision.HIGHEST
    stacked = jnp.concatenate([mask_rows, em_rows[:, None, :]], axis=1)
    cells = stacked.reshape(rows_here, 3, side_half, 2, side_half, 2 * CS)
    features = jnp.concatenate(
        [
            cells[:, channel, :, half].reshape(rows_here * side_half * side_half, 2 * CS)
            for channel in range(3)
            for half in range(2)
        ],
        axis=1,
    )
    pool_sum, weight_sum = conv_layers(features, patch_weight, conv_weight, conv_bias)
    pooled = jnp.sum(pool_sum.reshape(rows_here, side_half, channels), axis=1)
    total_weight = jnp.sum(weight_sum.reshape(rows_here, side_half, channels)[:, :, 0], axis=1)
    pooled = pooled / total_weight[:, None]
    logits = jnp.dot(pooled, score_weight, precision=highest)
    scores = jax.nn.sigmoid(logits).astype(jnp.bfloat16)
    embedded = jnp.tanh(jnp.dot(pooled, embed_weight.astype(jnp.float32), precision=highest))
    contrib = (scores.astype(jnp.float32)[:, None] * embedded).astype(jnp.bfloat16)
    return (scores, contrib)


def per_device(
    em_cutouts,
    mask_cutouts,
    live_count,
    segment_ids,
    patch_weight,
    conv_weight,
    conv_bias,
    score_weight,
    embed_weight,
):
    bulk_index = lax.axis_index("bulk")
    seg_index = lax.axis_index("seg")
    slots = em_cutouts.shape[2]
    em_local = em_cutouts.reshape(slots, -1)
    mask_local = mask_cutouts.reshape(slots, 2, -1)
    own_count = live_count[bulk_index, seg_index]
    slot_ids = jnp.arange(slots, dtype=jnp.int32)
    live_slot = slot_ids < own_count
    part_score, part_contrib = run_network(
        em_local, mask_local, patch_weight, conv_weight, conv_bias, score_weight, embed_weight
    )
    scores = jnp.where(live_slot, part_score, 0)
    contribs = jnp.where(live_slot[:, None], part_contrib, 0)
    n_seg = lax.axis_size("seg")
    seg_local = jnp.where(live_slot, segment_ids.reshape(slots), -1)
    segment_row = jnp.arange(n_seg * SEG_DEV, dtype=jnp.int32)
    onehot = (segment_row[:, None] == seg_local[None, :]).astype(jnp.bfloat16)
    partial_value = jnp.dot(onehot, contribs, preferred_element_type=jnp.float32)
    partial_value = partial_value.reshape(n_seg, SEG_DEV, -1)
    arrived = lax.all_to_all(partial_value, "seg", 0, 0, tiled=True)
    summed = jnp.sum(arrived, axis=0)
    return (scores.reshape(1, 1, slots), summed)


def solution(mesh):
    in_specs = (
        P("bulk", "seg", None, None),
        P("bulk", "seg", None, None, None),
        P(),
        P("bulk", "seg", None),
        P(),
        P(),
        P(),
        P(),
        P(),
    )
    out_specs = (P("bulk", "seg", None), P(("bulk", "seg"), None))
    return jax.shard_map(
        per_device, mesh=mesh, in_specs=in_specs, out_specs=out_specs, check_vma=False
    )
```

```python
import jax
import jax.numpy as jnp
from jax import lax
from jax.sharding import PartitionSpec as P
from jax.experimental import pallas as pl
from jax.experimental.pallas import tpu as pltpu

CS = 16
LAYERS = 3
SEG_DEV = 8
BLOCK_PAIRS = 8
PAD_ROWS = 16


def conv_kernel(
    x_ref, q_ref, first_bias_ref, w_ref, b_ref, pool_ref, weight_ref, pad_ref, col_ref, band_ref,
    tiled_ref,
):
    rows, lanes = pad_ref.shape[0] - 2 * PAD_ROWS, pad_ref.shape[1]
    side = CS // 2
    channels = w_ref.shape[2]
    edge = PAD_ROWS

    @pl.when(pl.program_id(0) == 0)
    def _():
        out_lane = lax.broadcasted_iota(jnp.int32, (channels, lanes), 1)
        in_row = lax.broadcasted_iota(jnp.int32, (channels, lanes), 0)
        spread = (out_lane % channels == in_row).astype(jnp.bfloat16)
        z_lane = out_lane // channels
        all_taps = w_ref[...].reshape(LAYERS * 27 * channels, channels)
        tiled_ref[...] = jnp.dot(all_taps, spread, preferred_element_type=jnp.float32)
        for layer_index in range(LAYERS):
            for tap in range(9):
                tiled = []
                for shift_c in range(3):
                    first_row = ((layer_index * 9 + tap) * 3 + shift_c) * channels
                    tiled.append(tiled_ref[first_row:first_row + channels, :])
                for z_in in range(side):
                    block = jnp.where(
                        z_lane == z_in + 1,
                        tiled[0],
                        jnp.where(
                            z_lane == z_in,
                            tiled[1],
                            jnp.where(z_lane == z_in - 1, tiled[2], 0.0),
                        ),
                    )
                    start = tap * lanes + z_in * channels
                    band_ref[layer_index, start:start + channels, :] = block.astype(jnp.bfloat16)

    pad_ref[0:edge, :] = jnp.zeros((edge, lanes), jnp.float32)
    pad_ref[edge + rows:, :] = jnp.zeros((edge, lanes), jnp.float32)
    first = jnp.dot(x_ref[...], q_ref[...], preferred_element_type=jnp.float32)
    first = jnp.maximum(first + first_bias_ref[...], 0.0).astype(jnp.bfloat16)
    pad_ref[edge:edge + rows, :] = first.astype(jnp.float32)
    row_id = lax.broadcasted_iota(jnp.int32, (rows, 1), 0)
    y_pos = row_id % side
    x_pos = (row_id // side) % side
    for layer_index in range(LAYERS):
        for shift_a in range(3):
            for shift_b in range(3):
                tap = shift_a * 3 + shift_b
                offset = (shift_a - 1) * side + (shift_b - 1)
                window = pad_ref[edge + offset:edge + offset + rows, :]
                x_to = x_pos + (shift_a - 1)
                y_to = y_pos + (shift_b - 1)
                inside = (x_to >= 0) & (x_to < side) & (y_to >= 0) & (y_to < side)
                col_ref[:, tap * lanes:(tap + 1) * lanes] = jnp.where(
                    inside, window, 0.0
                ).astype(jnp.bfloat16)
        summed = jnp.dot(col_ref[...], band_ref[layer_index], preferred_element_type=jnp.float32)
        hidden = jnp.maximum(summed + b_ref[layer_index], 0.0).astype(jnp.bfloat16)
        pad_ref[edge:edge + rows, :] = hidden.astype(jnp.float32)
    masks = x_ref[:, 0:128].astype(jnp.float32)
    overlap = masks * pltpu.roll(masks, 64, 1)
    over_hi = overlap.astype(jnp.bfloat16)
    over_lo = (overlap - over_hi.astype(jnp.float32)).astype(jnp.bfloat16)
    cell = lax.broadcasted_iota(jnp.int32, (128, lanes), 0)
    z_of_lane = lax.broadcasted_iota(jnp.int32, (128, lanes), 1) // channels
    gather = ((cell < 64) & ((cell // 2) % side == z_of_lane)).astype(jnp.bfloat16)
    cell_sum = jnp.dot(over_hi, gather, preferred_element_type=jnp.float32) + jnp.dot(
        over_lo, gather, preferred_element_type=jnp.float32
    )
    boundary = cell_sum * 0.125 + 0.1
    final = pad_ref[edge:edge + rows, :]
    pairs = rows // (side * side)
    pool_ref[...] = jnp.sum((final * boundary).reshape(pairs, side * side, lanes), axis=1)
    weight_ref[...] = jnp.sum(boundary.reshape(pairs, side * side, lanes), axis=1)


def conv_layers(features, patch_weight, conv_weight, conv_bias):
    total_rows, feature_count = features.shape
    side = CS // 2
    channels = conv_weight.shape[2]
    lanes = side * channels
    per_cell = patch_weight.reshape(channels, 3, 2, 2, 2).transpose(1, 2, 3, 4, 0)[
        jnp.array([1, 2, 0])
    ]
    z_in = jnp.arange(side)[:, None, None, None]
    z_out = jnp.arange(side)[None, None, :, None]
    patch_matrix = jnp.where(
        z_in == z_out, per_cell[:, :, :, None, :, None, :], 0
    ).reshape(feature_count, lanes)
    first_bias = jnp.tile(conv_bias[0], side).reshape(1, lanes)
    taps = conv_weight.transpose(0, 1, 3, 2)
    bias = jnp.tile(conv_bias[1:], (1, side)).reshape(LAYERS, 1, lanes)
    block_rows = BLOCK_PAIRS * side * side
    return pl.pallas_call(
        conv_kernel,
        grid=(total_rows // block_rows,),
        in_specs=[
            pl.BlockSpec((block_rows, feature_count), lambda i: (i, 0)),
            pl.BlockSpec((feature_count, lanes), lambda i: (0, 0)),
            pl.BlockSpec((1, lanes), lambda i: (0, 0)),
            pl.BlockSpec((LAYERS, 27, channels, channels), lambda i: (0, 0, 0, 0)),
            pl.BlockSpec((LAYERS, 1, lanes), lambda i: (0, 0, 0)),
        ],
        out_specs=[
            pl.BlockSpec((BLOCK_PAIRS, lanes), lambda i: (i, 0)),
            pl.BlockSpec((BLOCK_PAIRS, lanes), lambda i: (i, 0)),
        ],
        out_shape=[
            jax.ShapeDtypeStruct((total_rows // (side * side), lanes), jnp.float32),
            jax.ShapeDtypeStruct((total_rows // (side * side), lanes), jnp.float32),
        ],
        scratch_shapes=[
            pltpu.VMEM((block_rows + 2 * PAD_ROWS, lanes), jnp.float32),
            pltpu.VMEM((block_rows, 9 * lanes), jnp.bfloat16),
            pltpu.VMEM((LAYERS, 9 * lanes, lanes), jnp.bfloat16),
            pltpu.VMEM((LAYERS * 27 * channels, lanes), jnp.float32),
        ],
        compiler_params=pltpu.CompilerParams(dimension_semantics=("arbitrary",)),
    )(features, patch_matrix, first_bias, taps, bias)


def run_network(
    em_rows, mask_rows, patch_weight, conv_weight, conv_bias, score_weight, embed_weight
):
    rows_here = em_rows.shape[0]
    side_half = CS // 2
    voxel_count = side_half * side_half * side_half
    channels = conv_weight.shape[2]
    lanes = side_half * channels
    highest = lax.Precision.HIGHEST
    stacked = jnp.concatenate([mask_rows, em_rows[:, None, :]], axis=1)
    cells = stacked.reshape(rows_here, 3, side_half, 2, side_half, 2 * CS)
    features = jnp.concatenate(
        [
            cells[:, channel, :, half].reshape(rows_here * side_half * side_half, 2 * CS)
            for channel in range(3)
            for half in range(2)
        ],
        axis=1,
    )
    pool_sum, weight_sum = conv_layers(features, patch_weight, conv_weight, conv_bias)
    pooled = jnp.sum(pool_sum.reshape(rows_here, side_half, channels), axis=1)
    total_weight = jnp.sum(weight_sum.reshape(rows_here, side_half, channels)[:, :, 0], axis=1)
    pooled = pooled / total_weight[:, None]
    logits = jnp.dot(pooled, score_weight, precision=highest)
    scores = jax.nn.sigmoid(logits).astype(jnp.bfloat16)
    embedded = jnp.tanh(jnp.dot(pooled, embed_weight.astype(jnp.float32), precision=highest))
    contrib = (scores.astype(jnp.float32)[:, None] * embedded).astype(jnp.bfloat16)
    return (scores, contrib)


def per_device(
    em_cutouts,
    mask_cutouts,
    live_count,
    segment_ids,
    patch_weight,
    conv_weight,
    conv_bias,
    score_weight,
    embed_weight,
):
    bulk_index = lax.axis_index("bulk")
    seg_index = lax.axis_index("seg")
    slots = em_cutouts.shape[2]
    em_local = em_cutouts.reshape(slots, -1)
    mask_local = mask_cutouts.reshape(slots, 2, -1)
    own_count = live_count[bulk_index, seg_index]
    slot_ids = jnp.arange(slots, dtype=jnp.int32)
    live_slot = slot_ids < own_count
    part_score, part_contrib = run_network(
        em_local, mask_local, patch_weight, conv_weight, conv_bias, score_weight, embed_weight
    )
    scores = jnp.where(live_slot, part_score, 0)
    contribs = jnp.where(live_slot[:, None], part_contrib, 0)
    n_seg = lax.axis_size("seg")
    seg_local = jnp.where(live_slot, segment_ids.reshape(slots), -1)
    segment_row = jnp.arange(n_seg * SEG_DEV, dtype=jnp.int32)
    onehot = (segment_row[:, None] == seg_local[None, :]).astype(jnp.bfloat16)
    partial_value = jnp.dot(onehot, contribs, preferred_element_type=jnp.float32)
    partial_value = partial_value.reshape(n_seg, SEG_DEV, -1)
    arrived = lax.all_to_all(partial_value, "seg", 0, 0, tiled=True)
    summed = jnp.sum(arrived, axis=0)
    return (scores.reshape(1, 1, slots), summed)


def solution(mesh):
    in_specs = (
        P("bulk", "seg", None, None),
        P("bulk", "seg", None, None, None),
        P(),
        P("bulk", "seg", None),
        P(),
        P(),
        P(),
        P(),
        P(),
    )
    out_specs = (P("bulk", "seg", None), P(("bulk", "seg"), None))
    return jax.shard_map(
        per_device, mesh=mesh, in_specs=in_specs, out_specs=out_specs, check_vma=False
    )
```

```python
import jax
import jax.numpy as jnp
from jax import lax
from jax.sharding import PartitionSpec as P
from jax.experimental import pallas as pl
from jax.experimental.pallas import tpu as pltpu

CS = 16
LAYERS = 3
SEG_DEV = 8
BLOCK_PAIRS = 40
PAD_ROWS = 16


def conv_kernel(
    x_ref, q_ref, first_bias_ref, w_ref, b_ref, pool_ref, weight_ref, pad_ref, col_ref, band_ref,
    tiled_ref,
):
    rows, lanes = pad_ref.shape[0] - 2 * PAD_ROWS, pad_ref.shape[1]
    side = CS // 2
    channels = w_ref.shape[2]
    edge = PAD_ROWS

    @pl.when(pl.program_id(0) == 0)
    def _():
        out_lane = lax.broadcasted_iota(jnp.int32, (channels, lanes), 1)
        in_row = lax.broadcasted_iota(jnp.int32, (channels, lanes), 0)
        spread = (out_lane % channels == in_row).astype(jnp.bfloat16)
        z_lane = out_lane // channels
        all_taps = w_ref[...].reshape(LAYERS * 27 * channels, channels)
        tiled_ref[...] = jnp.dot(all_taps, spread, preferred_element_type=jnp.float32)
        for layer_index in range(LAYERS):
            for tap in range(9):
                tiled = []
                for shift_c in range(3):
                    first_row = ((layer_index * 9 + tap) * 3 + shift_c) * channels
                    tiled.append(tiled_ref[first_row:first_row + channels, :])
                for z_in in range(side):
                    block = jnp.where(
                        z_lane == z_in + 1,
                        tiled[0],
                        jnp.where(
                            z_lane == z_in,
                            tiled[1],
                            jnp.where(z_lane == z_in - 1, tiled[2], 0.0),
                        ),
                    )
                    start = tap * lanes + z_in * channels
                    band_ref[layer_index, start:start + channels, :] = block.astype(jnp.bfloat16)

    pad_ref[0:edge, :] = jnp.zeros((edge, lanes), jnp.float32)
    pad_ref[edge + rows:, :] = jnp.zeros((edge, lanes), jnp.float32)
    first = jnp.dot(x_ref[...], q_ref[...], preferred_element_type=jnp.float32)
    first = jnp.maximum(first + first_bias_ref[...], 0.0).astype(jnp.bfloat16)
    pad_ref[edge:edge + rows, :] = first.astype(jnp.float32)
    row_id = lax.broadcasted_iota(jnp.int32, (rows, 1), 0)
    y_pos = row_id % side
    x_pos = (row_id // side) % side
    for layer_index in range(LAYERS):
        for shift_a in range(3):
            for shift_b in range(3):
                tap = shift_a * 3 + shift_b
                offset = (shift_a - 1) * side + (shift_b - 1)
                window = pad_ref[edge + offset:edge + offset + rows, :]
                x_to = x_pos + (shift_a - 1)
                y_to = y_pos + (shift_b - 1)
                inside = (x_to >= 0) & (x_to < side) & (y_to >= 0) & (y_to < side)
                col_ref[:, tap * lanes:(tap + 1) * lanes] = jnp.where(
                    inside, window, 0.0
                ).astype(jnp.bfloat16)
        summed = jnp.dot(col_ref[...], band_ref[layer_index], preferred_element_type=jnp.float32)
        hidden = jnp.maximum(summed + b_ref[layer_index], 0.0).astype(jnp.bfloat16)
        pad_ref[edge:edge + rows, :] = hidden.astype(jnp.float32)
    masks = x_ref[:, 0:128].astype(jnp.float32)
    overlap = masks * pltpu.roll(masks, 64, 1)
    over_hi = overlap.astype(jnp.bfloat16)
    over_lo = (overlap - over_hi.astype(jnp.float32)).astype(jnp.bfloat16)
    cell = lax.broadcasted_iota(jnp.int32, (128, lanes), 0)
    z_of_lane = lax.broadcasted_iota(jnp.int32, (128, lanes), 1) // channels
    gather = ((cell < 64) & ((cell // 2) % side == z_of_lane)).astype(jnp.bfloat16)
    cell_sum = jnp.dot(over_hi, gather, preferred_element_type=jnp.float32) + jnp.dot(
        over_lo, gather, preferred_element_type=jnp.float32
    )
    boundary = cell_sum * 0.125 + 0.1
    final = pad_ref[edge:edge + rows, :]
    pairs = rows // (side * side)
    pool_ref[...] = jnp.sum((final * boundary).reshape(pairs, side * side, lanes), axis=1)
    weight_ref[...] = jnp.sum(boundary.reshape(pairs, side * side, lanes), axis=1)


def conv_layers(features, patch_weight, conv_weight, conv_bias):
    total_rows, feature_count = features.shape
    side = CS // 2
    channels = conv_weight.shape[2]
    lanes = side * channels
    per_cell = patch_weight.reshape(channels, 3, 2, 2, 2).transpose(1, 2, 3, 4, 0)[
        jnp.array([1, 2, 0])
    ]
    z_in = jnp.arange(side)[:, None, None, None]
    z_out = jnp.arange(side)[None, None, :, None]
    patch_matrix = jnp.where(
        z_in == z_out, per_cell[:, :, :, None, :, None, :], 0
    ).reshape(feature_count, lanes)
    first_bias = jnp.tile(conv_bias[0], side).reshape(1, lanes)
    taps = conv_weight.transpose(0, 1, 3, 2)
    bias = jnp.tile(conv_bias[1:], (1, side)).reshape(LAYERS, 1, lanes)
    block_rows = BLOCK_PAIRS * side * side
    return pl.pallas_call(
        conv_kernel,
        grid=(total_rows // block_rows,),
        in_specs=[
            pl.BlockSpec((block_rows, feature_count), lambda i: (i, 0)),
            pl.BlockSpec((feature_count, lanes), lambda i: (0, 0)),
            pl.BlockSpec((1, lanes), lambda i: (0, 0)),
            pl.BlockSpec((LAYERS, 27, channels, channels), lambda i: (0, 0, 0, 0)),
            pl.BlockSpec((LAYERS, 1, lanes), lambda i: (0, 0, 0)),
        ],
        out_specs=[
            pl.BlockSpec((BLOCK_PAIRS, lanes), lambda i: (i, 0)),
            pl.BlockSpec((BLOCK_PAIRS, lanes), lambda i: (i, 0)),
        ],
        out_shape=[
            jax.ShapeDtypeStruct((total_rows // (side * side), lanes), jnp.float32),
            jax.ShapeDtypeStruct((total_rows // (side * side), lanes), jnp.float32),
        ],
        scratch_shapes=[
            pltpu.VMEM((block_rows + 2 * PAD_ROWS, lanes), jnp.float32),
            pltpu.VMEM((block_rows, 9 * lanes), jnp.bfloat16),
            pltpu.VMEM((LAYERS, 9 * lanes, lanes), jnp.bfloat16),
            pltpu.VMEM((LAYERS * 27 * channels, lanes), jnp.float32),
        ],
        compiler_params=pltpu.CompilerParams(dimension_semantics=("arbitrary",)),
    )(features, patch_matrix, first_bias, taps, bias)


def run_network(
    em_rows, mask_rows, patch_weight, conv_weight, conv_bias, score_weight, embed_weight
):
    rows_here = em_rows.shape[0]
    side_half = CS // 2
    voxel_count = side_half * side_half * side_half
    channels = conv_weight.shape[2]
    lanes = side_half * channels
    highest = lax.Precision.HIGHEST
    stacked = jnp.concatenate([mask_rows, em_rows[:, None, :]], axis=1)
    cells = stacked.reshape(rows_here, 3, side_half, 2, side_half, 2 * CS)
    features = jnp.concatenate(
        [
            cells[:, channel, :, half].reshape(rows_here * side_half * side_half, 2 * CS)
            for channel in range(3)
            for half in range(2)
        ],
        axis=1,
    )
    pool_sum, weight_sum = conv_layers(features, patch_weight, conv_weight, conv_bias)
    pooled = jnp.sum(pool_sum.reshape(rows_here, side_half, channels), axis=1)
    total_weight = jnp.sum(weight_sum.reshape(rows_here, side_half, channels)[:, :, 0], axis=1)
    pooled = pooled / total_weight[:, None]
    logits = jnp.dot(pooled, score_weight, precision=highest)
    scores = jax.nn.sigmoid(logits).astype(jnp.bfloat16)
    embedded = jnp.tanh(jnp.dot(pooled, embed_weight.astype(jnp.float32), precision=highest))
    contrib = (scores.astype(jnp.float32)[:, None] * embedded).astype(jnp.bfloat16)
    return (scores, contrib)


def per_device(
    em_cutouts,
    mask_cutouts,
    live_count,
    segment_ids,
    patch_weight,
    conv_weight,
    conv_bias,
    score_weight,
    embed_weight,
):
    bulk_index = lax.axis_index("bulk")
    seg_index = lax.axis_index("seg")
    slots = em_cutouts.shape[2]
    em_local = em_cutouts.reshape(slots, -1)
    mask_local = mask_cutouts.reshape(slots, 2, -1)
    own_count = live_count[bulk_index, seg_index]
    slot_ids = jnp.arange(slots, dtype=jnp.int32)
    live_slot = slot_ids < own_count
    part_score, part_contrib = run_network(
        em_local, mask_local, patch_weight, conv_weight, conv_bias, score_weight, embed_weight
    )
    scores = jnp.where(live_slot, part_score, 0)
    contribs = jnp.where(live_slot[:, None], part_contrib, 0)
    n_seg = lax.axis_size("seg")
    seg_local = jnp.where(live_slot, segment_ids.reshape(slots), -1)
    segment_row = jnp.arange(n_seg * SEG_DEV, dtype=jnp.int32)
    onehot = (segment_row[:, None] == seg_local[None, :]).astype(jnp.bfloat16)
    partial_value = jnp.dot(onehot, contribs, preferred_element_type=jnp.float32)
    partial_value = partial_value.reshape(n_seg, SEG_DEV, -1)
    arrived = lax.all_to_all(partial_value, "seg", 0, 0, tiled=True)
    summed = jnp.sum(arrived, axis=0)
    return (scores.reshape(1, 1, slots), summed)


def solution(mesh):
    in_specs = (
        P("bulk", "seg", None, None),
        P("bulk", "seg", None, None, None),
        P(),
        P("bulk", "seg", None),
        P(),
        P(),
        P(),
        P(),
        P(),
    )
    out_specs = (P("bulk", "seg", None), P(("bulk", "seg"), None))
    return jax.shard_map(
        per_device, mesh=mesh, in_specs=in_specs, out_specs=out_specs, check_vma=False
    )
```
